32 devices in a mesh: seq: 4 (over y, x), vocab: 8 (over z, core).
Axes of the slice: x: 2, y: 2, z: 4, core: 2. Of those that a mesh axis runs over, the one named last changes fastest.
Arguments:
- pre_query: bfloat16 [8, 2048, 2560], P('vocab', 'seq')
- pre_fresh: bfloat16 [8, 2048, 512], P('vocab', 'seq'), may hold values from -6 to 6
- pre_cache: bfloat16 [8, 2048, 512], P('vocab', 'seq'), may hold values from -6 to 6
- pre_start: int32 [8], P('vocab'), may hold values from 0 to 6143
- pre_resid: bfloat16 [8, 2048, 2560], P('vocab', 'seq'), may hold values from -0.75 to 0.75
- dec_query: bfloat16 [32, 2560], P(('seq', 'vocab'))
- dec_fresh: bfloat16 [32, 512], P(('seq', 'vocab')), may hold values from -6 to 6
- decode_window_cache: bfloat16 [32, 2048, 512], P(('seq', 'vocab')), may hold values from -6 to 6
- dec_length: int32 [32], P(('seq', 'vocab')), may hold values from 1 to 8192
- dec_resid: bfloat16 [32, 2560], P(('seq', 'vocab')), may hold values from -0.75 to 0.75
- out_weight: bfloat16 [2560, 2560], P('vocab'), may hold values from -0.125 to 0.125
- norm_gain: float32 [2560], replicated, may hold values from 0.5 to 1.5
- embedding: bfloat16 [256000, 2560], P(('seq', 'vocab'))
Outputs:
- pre_out: bfloat16 [8, 2048, 2560], P('vocab', 'seq')
- dec_out: bfloat16 [32, 2560], P(('seq', 'vocab'))
- dec_logp: bfloat16 [32, 256000], P(None, ('seq', 'vocab'))
- pre_logp: bfloat16 [8, 256000], P(None, ('seq', 'vocab'))
The draws below stay inside these ranges and needn't reach their ends.
All inputs are finite; a program needn't handle non-finite values.
Results may differ from the reference program's by a relative error of at most 0.0065.
Values may be sent and summed in bfloat16 or wider, within the bound.
No kernel may reach another device: no remote copies, remote signals or barrier semaphores. Data moves between devices by JAX's collectives and lax.ppermute only.
A program may use at most 320 MiB of HBM per device.

```python
import math
import jax
import jax.numpy as jnp
from jax import lax

D = 2560
HQ = 10
HEAD_SIZE = 256
WIN = 2048
VOCAB = 256000
SPAN = 2048
PRE = 8
DEC = 32


def query_values(key, shape):
    values = jax.random.normal(jax.random.fold_in(key, 11), shape, jnp.float32)
    return values


def draw_pre_query(key, part):
    return query_values(key, (PRE, SPAN, HQ * HEAD_SIZE)).astype(jnp.bfloat16)


def draw_dec_query(key, part):
    return query_values(key, (DEC, HQ * HEAD_SIZE)).astype(jnp.bfloat16)


def draw_dec_length(key, part):
    longest = 4 * WIN
    top_power = longest.bit_length() - 1
    powers = jax.random.randint(jax.random.fold_in(key, 21), (DEC,), 2, top_power + 1)
    upper_len = jnp.minimum(2 ** powers, longest)
    lengths = jax.random.randint(jax.random.fold_in(key, 22), (DEC,), 1, upper_len + 1)
    chosen = jax.random.randint(jax.random.fold_in(key, 23), (), 0, DEC)
    return lengths.at[chosen].set(longest).astype(jnp.int32)


def draw_embedding(key, part):
    values = jax.random.normal(jax.random.fold_in(key, 31), (VOCAB, D), jnp.float32) * (3.0 / math.sqrt(D))
    return values.astype(jnp.bfloat16)


def place_ends(drawn, own_key, least, high):
    spot = [jax.random.randint(jax.random.fold_in(own_key, axis), (), 0, length) for axis, length in enumerate(drawn.shape)]
    widest = drawn.shape.index(max(drawn.shape))
    neighbour = spot[:widest] + [(spot[widest] + 1) % drawn.shape[widest]] + spot[widest + 1:]
    return drawn.at[tuple(spot)].set(least).at[tuple(neighbour)].set(high)


def block_scale(own_key, extent, split, least, top_value):
    level, own = 1.0, jax.random.fold_in(own_key, 6)
    for position, blocks in split:
        steps = jnp.exp(jax.random.uniform(jax.random.fold_in(own, position), (blocks,), jnp.float32, least / len(split), top_value / len(split)))
        level = level * jnp.repeat(steps, extent[position] // blocks).reshape([-1 if axis == position else 1 for axis in range(len(extent))])
    return level


def noise(rng, dims, width, most, cuts=(), kind=jnp.bfloat16):
    result = jax.random.normal(rng, dims, jnp.float32) * width
    if len(cuts) > 0:
        result = block_scale(rng, dims, cuts, -0.22, 0.18) * result
    return jnp.clip(result, min=-most, max=most).astype(kind)


def setup_inputs(seed: int = 0) -> dict:
    splits = jax.random.split(jax.random.key(seed), 14)
    pre_query = draw_pre_query(jax.random.fold_in(splits[13], 71), 0)
    pre_fresh = noise(splits[1], (PRE, SPAN, 2 * HEAD_SIZE), 1.0, 6.0, ((0, 8), (1, 4)))
    pre_cache = noise(splits[2], (PRE, WIN, 2 * HEAD_SIZE), 1.0, 6.0, ((0, 8), (1, 4)))
    pre_start = place_ends(jax.random.randint(splits[3], (PRE,), 0, 3 * WIN), jax.random.fold_in(splits[3], 1), 0, (3 * WIN) - 1).astype(jnp.int32)
    pre_resid = noise(splits[4], (PRE, SPAN, D), 0.05, 0.75, ((0, 8), (1, 4)))
    dec_query = draw_dec_query(jax.random.fold_in(splits[13], 71), 0)
    dec_fresh = noise(splits[6], (DEC, 2 * HEAD_SIZE), 1.0, 6.0, ((0, 32),))
    decode_window_cache = noise(splits[7], (DEC, WIN, 2 * HEAD_SIZE), 1.0, 6.0, ((0, 32),))
    dec_length = draw_dec_length(jax.random.fold_in(splits[13], 71), 0)
    dec_resid = noise(splits[9], (DEC, D), 0.05, 0.75, ((0, 32),))
    out_weight = noise(splits[10], (HQ * HEAD_SIZE, D), (HQ * HEAD_SIZE) ** -0.5, 0.125, ((0, 8),))
    norm_gain = jnp.clip(1.0 + 0.1 * jax.random.normal(splits[11], (D,), jnp.float32), 0.5, 1.5)
    embedding = draw_embedding(jax.random.fold_in(splits[13], 71), 0)
    return {"pre_query": pre_query, "pre_fresh": pre_fresh, "pre_cache": pre_cache, "pre_start": pre_start, "pre_resid": pre_resid, "dec_query": dec_query, "dec_fresh": dec_fresh, "decode_window_cache": decode_window_cache, "dec_length": dec_length, "dec_resid": dec_resid, "out_weight": out_weight, "norm_gain": norm_gain, "embedding": embedding}


NEG_BIG = -1e+30
STABILITY_FLOOR = 1e-06

def attend(scores, valid_mask, value_rows):
    peak_score = lax.optimization_barrier(jnp.max(jnp.where(valid_mask, scores, NEG_BIG), axis=1, keepdims=True))
    weights = jnp.where(valid_mask, jnp.exp(scores - peak_score), 0.0)
    denom_sum = lax.optimization_barrier(jnp.sum(weights, axis=1, keepdims=True))
    mixed_rows = jnp.dot(weights.astype(jnp.bfloat16), value_rows, preferred_element_type=jnp.float32) / denom_sum
    return mixed_rows.astype(jnp.bfloat16)

def prefill_single_request(inputs):
    query, fresh_kv, cached_kv, start = inputs
    query_rows = query.reshape(SPAN * HQ, HEAD_SIZE)
    key_rows = jnp.concatenate([cached_kv[:, :HEAD_SIZE], fresh_kv[:, :HEAD_SIZE]], axis=0)
    value_rows = jnp.concatenate([cached_kv[:, HEAD_SIZE:], fresh_kv[:, HEAD_SIZE:]], axis=0)
    scores = jnp.dot(query_rows, key_rows.T, preferred_element_type=jnp.float32) * HEAD_SIZE ** (-0.5)
    query_offset = (jnp.arange(SPAN * HQ, dtype=jnp.int32) // HQ)[:, None]
    key_offset = jnp.concatenate([jnp.arange(WIN, dtype=jnp.int32) - WIN, jnp.arange(SPAN, dtype=jnp.int32)])[None, :]
    valid_mask = (key_offset <= query_offset) & (query_offset - key_offset < WIN) & (start + key_offset >= 0)
    return attend(scores, valid_mask, value_rows).reshape(SPAN, HQ * HEAD_SIZE)

def decode_request(inputs):
    query, fresh_kv, cached_kv, length = inputs
    query_rows = query.reshape(HQ, HEAD_SIZE)
    key_rows = jnp.concatenate([cached_kv[:, :HEAD_SIZE], fresh_kv[None, :HEAD_SIZE]], axis=0)
    value_rows = jnp.concatenate([cached_kv[:, HEAD_SIZE:], fresh_kv[None, HEAD_SIZE:]], axis=0)
    scores = jnp.dot(query_rows, key_rows.T, preferred_element_type=jnp.float32) * HEAD_SIZE ** (-0.5)
    slot_index = jnp.arange(WIN, dtype=jnp.int32)
    held_pos = length - 1 - jnp.mod(length - 1 - slot_index, WIN)
    live_slots = (held_pos >= 0) & (held_pos > length - WIN)
    live_mask = jnp.concatenate([live_slots, jnp.ones((1,), dtype=bool)])[None, :]
    return attend(scores, live_mask, value_rows).reshape(HQ * HEAD_SIZE)

def normalize(rows_in, gain):
    values = rows_in.astype(jnp.float32)
    square_mean = lax.optimization_barrier(jnp.mean(values * values, axis=-1, keepdims=True))
    return (values * lax.rsqrt(square_mean + STABILITY_FLOOR) * gain).astype(jnp.bfloat16)

def reference(pre_query, pre_fresh, pre_cache, pre_start, pre_resid, dec_query, dec_fresh, decode_window_cache, dec_length, dec_resid, out_weight, norm_gain, embedding):
    pre_mixed = lax.map(prefill_single_request, (pre_query, pre_fresh, pre_cache, pre_start))
    dec_mixed = lax.map(decode_request, (dec_query, dec_fresh, decode_window_cache, dec_length))
    pre_proj = jnp.dot(pre_mixed.reshape(PRE * SPAN, HQ * HEAD_SIZE), out_weight, preferred_element_type=jnp.float32)
    pre_out = (pre_resid.astype(jnp.float32) + pre_proj.reshape(PRE, SPAN, D)).astype(jnp.bfloat16)
    dec_proj = jnp.dot(dec_mixed, out_weight, preferred_element_type=jnp.float32)
    dec_out = (dec_resid.astype(jnp.float32) + dec_proj).astype(jnp.bfloat16)
    head_in = jnp.concatenate([dec_out, pre_out[:, SPAN - 1, :]], axis=0)
    head_rows = normalize(head_in, norm_gain)
    logits = jnp.dot(head_rows, embedding.T, preferred_element_type=jnp.float32)
    peak_logit = lax.optimization_barrier(jnp.max(logits, axis=1, keepdims=True))
    total = peak_logit + jnp.log(lax.optimization_barrier(jnp.sum(jnp.exp(logits - peak_logit), axis=1, keepdims=True)))
    log_probs = (logits - total).astype(jnp.bfloat16)
    return (pre_out, dec_out, log_probs[:DEC], log_probs[DEC:])
```

```python
import functools

import jax
import jax.numpy as jnp
from jax import lax
from jax.experimental import pallas as pl
from jax.experimental.pallas import tpu as pltpu
from jax.sharding import PartitionSpec as P

D = 2560
HQ = 10
HEAD_SIZE = 256
WIN = 2048


NEG_BIG = -1e30
STABILITY_FLOOR = 1e-06


def from_behind(value, axis, steps):
    count = lax.axis_size(axis)
    pairs = [(source, (source + steps) % count) for source in range(count)]
    return lax.ppermute(value, axis, pairs)


def gather_all(value):
    inner = lax.all_gather(value, "vocab", axis=0, tiled=True)
    return lax.all_gather(inner, "seq", axis=0, tiled=True)


def normalize(rows_in, gain):
    values = rows_in.astype(jnp.float32)
    square_mean = jnp.mean(values * values, axis=-1, keepdims=True)
    return (values * lax.rsqrt(square_mean + STABILITY_FLOOR) * gain).astype(jnp.bfloat16)


def prefill_kernel(t0_ref, q_ref, *refs, n_blocks, block, tq):
    kv_refs = refs[:n_blocks]
    o_ref = refs[n_blocks]
    r = pl.program_id(0)
    qi = pl.program_id(2)
    t0 = t0_ref[r]
    q = q_ref[0]
    row = qi * tq + lax.broadcasted_iota(jnp.int32, (tq, block), 0)
    col = lax.broadcasted_iota(jnp.int32, (tq, block), 1)
    peak = jnp.full((tq, 1), NEG_BIG, jnp.float32)
    denom = jnp.zeros((tq, 1), jnp.float32)
    accum = jnp.zeros((tq, HEAD_SIZE), jnp.float32)
    scale = HEAD_SIZE ** (-0.5)
    for j in range(n_blocks):
        kv = kv_refs[j]
        keys = kv[0, :, :HEAD_SIZE]
        values = kv[0, :, HEAD_SIZE:]
        scores = (
            lax.dot_general(
                q, keys, (((1,), (1,)), ((), ())), preferred_element_type=jnp.float32
            )
            * scale
        )
        t = j * block + col
        valid = t >= t0
        if j == 0:
            valid = valid & (t > row)
        if j == n_blocks - 1:
            valid = valid & (t <= row + WIN)
        peak_new = jnp.maximum(
            peak, jnp.max(jnp.where(valid, scores, NEG_BIG), axis=1, keepdims=True)
        )
        weights = jnp.where(valid, jnp.exp(scores - peak_new), 0.0)
        decay = jnp.exp(peak - peak_new)
        denom = denom * decay + jnp.sum(weights, axis=1, keepdims=True)
        accum = accum * decay + jnp.dot(
            weights.astype(jnp.bfloat16), values, preferred_element_type=jnp.float32
        )
        peak = peak_new
    o_ref[0] = (accum / denom).astype(o_ref.dtype)


def prefill_attention(pre_query, kv_blocks, first_key):
    local_pre, block_query, _ = pre_query.shape
    block = kv_blocks[0].shape[1]
    n_blocks = len(kv_blocks)
    tq = min(block_query, 512)
    kernel = functools.partial(prefill_kernel, n_blocks=n_blocks, block=block, tq=tq)
    kv_spec = pl.BlockSpec((1, block, 2 * HEAD_SIZE), lambda r, h, qi, t0: (r, 0, 0))
    q_spec = pl.BlockSpec((1, tq, HEAD_SIZE), lambda r, h, qi, t0: (r, qi, h))
    flops = 4 * local_pre * HQ * block_query * block * n_blocks * HEAD_SIZE
    return pl.pallas_call(
        kernel,
        out_shape=jax.ShapeDtypeStruct(pre_query.shape, jnp.bfloat16),
        grid_spec=pltpu.PrefetchScalarGridSpec(
            num_scalar_prefetch=1,
            grid=(local_pre, HQ, block_query // tq),
            in_specs=[q_spec] + [kv_spec] * n_blocks,
            out_specs=q_spec,
        ),
        compiler_params=pltpu.CompilerParams(
            dimension_semantics=("arbitrary", "arbitrary", "arbitrary")
        ),
        cost_estimate=pl.CostEstimate(
            flops=flops,
            transcendentals=local_pre * HQ * block_query * block * n_blocks,
            bytes_accessed=2 * pre_query.size * 2 + sum(b.size for b in kv_blocks) * 2,
        ),
    )(first_key, pre_query, *kv_blocks)


def body(
    pre_query,
    pre_fresh,
    pre_cache,
    pre_start,
    pre_resid,
    dec_query,
    dec_fresh,
    decode_window_cache,
    dec_length,
    dec_resid,
    out_weight,
    norm_gain,
    embedding,
):
    seq_count = lax.axis_size("seq")
    seq_index = lax.axis_index("seq")
    local_pre = pre_query.shape[0]
    block_query = pre_query.shape[1]
    score_scale = HEAD_SIZE ** (-0.5)
    kv_blocks = [None] * (seq_count + 1)
    kv_blocks[0] = pre_cache
    kv_blocks[seq_count] = pre_fresh
    for shift in range(1, seq_count):
        outgoing = jnp.where(seq_index + shift <= seq_count - 1, pre_fresh, pre_cache)
        kv_blocks[seq_count - shift] = from_behind(outgoing, "seq", shift)
    first_key = (WIN - seq_index * block_query - pre_start).astype(jnp.int32)
    pre_mixed = prefill_attention(pre_query, kv_blocks, first_key).reshape(
        local_pre * block_query, HQ * HEAD_SIZE
    )
    decode_token_rows = dec_query.reshape(-1, HQ, HEAD_SIZE)
    cache_scores = (
        jnp.einsum(
            "vfx,vzx->vfz",
            decode_token_rows,
            decode_window_cache[:, :, :HEAD_SIZE],
            preferred_element_type=jnp.float32,
        )
        * score_scale
    )
    self_scores = (
        jnp.einsum(
            "bhd,bd->bh",
            decode_token_rows,
            dec_fresh[:, :HEAD_SIZE],
            preferred_element_type=jnp.float32,
        )[:, :, None]
        * score_scale
    )
    slot_index = jnp.arange(WIN, dtype=jnp.int32)[None, :]
    length_col = dec_length[:, None]
    held_pos = length_col - 1 - jnp.mod(length_col - 1 - slot_index, WIN)
    live_mask = ((held_pos >= 0) & (held_pos > length_col - WIN))[:, None, :]
    peak_score = jnp.maximum(
        jnp.max(jnp.where(live_mask, cache_scores, NEG_BIG), axis=2, keepdims=True), self_scores
    )
    cache_attention_weights = jnp.where(live_mask, jnp.exp(cache_scores - peak_score), 0.0)
    self_weights = jnp.exp(self_scores - peak_score)
    denom_sum = jnp.sum(cache_attention_weights, axis=2, keepdims=True) + self_weights
    self_rounded = lax.optimization_barrier(self_weights.astype(jnp.bfloat16)).astype(jnp.float32)
    cache_part = jnp.einsum(
        "ect,ety->ecy",
        cache_attention_weights.astype(jnp.bfloat16),
        decode_window_cache[:, :, HEAD_SIZE:],
        preferred_element_type=jnp.float32,
    )
    self_part = self_rounded * dec_fresh[:, None, HEAD_SIZE:].astype(jnp.float32)
    dec_mixed = (
        ((cache_part + self_part) / denom_sum).astype(jnp.bfloat16).reshape(-1, HQ * HEAD_SIZE)
    )
    mixed_rows = jnp.concatenate([pre_mixed, dec_mixed], axis=0)
    projected = jnp.dot(
        mixed_rows,
        lax.all_gather(out_weight, "vocab", axis=0, tiled=True),
        preferred_element_type=jnp.float32,
    )
    pre_rows = local_pre * block_query
    pre_out = (
        pre_resid.astype(jnp.float32) + projected[:pre_rows].reshape(local_pre, block_query, D)
    ).astype(jnp.bfloat16)
    dec_out = (dec_resid.astype(jnp.float32) + projected[pre_rows:]).astype(jnp.bfloat16)
    head_decode = normalize(dec_out, norm_gain)
    head_prefill = normalize(pre_out[:, block_query - 1, :], norm_gain)
    local_dec = head_decode.shape[0]
    vocab_count = lax.axis_size("vocab")
    local_head = jnp.concatenate([head_decode, head_prefill], axis=0)
    everyone = gather_all(local_head)
    layout = everyone.reshape(seq_count, vocab_count, local_dec + local_pre, D)
    decode_all = layout[:, :, :local_dec].reshape(-1, D)
    prefill_every_request = layout[seq_count - 1, :, local_dec:].reshape(-1, D)
    head_rows = jnp.concatenate([decode_all, prefill_every_request], axis=0)
    logits = lax.dot_general(
        head_rows, embedding, (((1,), (1,)), ((), ())), preferred_element_type=jnp.float32
    )
    local_peak = jnp.max(logits, axis=1)
    local_sum = jnp.sum(jnp.exp(logits - local_peak[:, None]), axis=1)
    stats = gather_all(jnp.stack([local_peak, local_sum])[None])
    global_peak = jnp.max(stats[:, 0], axis=0)
    global_sum = jnp.sum(stats[:, 1] * jnp.exp(stats[:, 0] - global_peak[None]), axis=0)
    total = (global_peak + jnp.log(global_sum))[:, None]
    log_probs = (logits - total).astype(jnp.bfloat16)
    dec_count = decode_all.shape[0]
    return (pre_out, dec_out, log_probs[:dec_count], log_probs[dec_count:])


def solution(mesh):
    in_specs = (
        P("vocab", "seq", None),
        P("vocab", "seq", None),
        P("vocab", "seq", None),
        P("vocab"),
        P("vocab", "seq", None),
        P(("seq", "vocab"), None),
        P(("seq", "vocab"), None),
        P(("seq", "vocab"), None, None),
        P(("seq", "vocab")),
        P(("seq", "vocab"), None),
        P("vocab", None),
        P(),
        P(("seq", "vocab"), None),
    )
    out_specs = (
        P("vocab", "seq", None),
        P(("seq", "vocab"), None),
        P(None, ("seq", "vocab")),
        P(None, ("seq", "vocab")),
    )
    return jax.shard_map(body, mesh=mesh, in_specs=in_specs, out_specs=out_specs, check_vma=False)
```

```python
import functools

import jax
import jax.numpy as jnp
from jax import lax
from jax.experimental import pallas as pl
from jax.experimental.pallas import tpu as pltpu
from jax.sharding import PartitionSpec as P

D = 2560
HQ = 10
HEAD_SIZE = 256
WIN = 2048


NEG_BIG = -1e30
STABILITY_FLOOR = 1e-06


def from_behind(value, axis, steps):
    count = lax.axis_size(axis)
    pairs = [(source, (source + steps) % count) for source in range(count)]
    return lax.ppermute(value, axis, pairs)


def gather_all(value):
    inner = lax.all_gather(value, "vocab", axis=0, tiled=True)
    return lax.all_gather(inner, "seq", axis=0, tiled=True)


def normalize(rows_in, gain):
    values = rows_in.astype(jnp.float32)
    square_mean = jnp.mean(values * values, axis=-1, keepdims=True)
    return (values * lax.rsqrt(square_mean + STABILITY_FLOOR) * gain).astype(jnp.bfloat16)


def prefill_kernel(t0_ref, q_ref, *refs, n_blocks, block, tq):
    kv_refs = refs[:n_blocks]
    o_ref = refs[n_blocks]
    r = pl.program_id(0)
    qi = pl.program_id(2)
    t0 = t0_ref[r]
    q = q_ref[0]
    row = qi * tq + lax.broadcasted_iota(jnp.int32, (tq, block), 0)
    col = lax.broadcasted_iota(jnp.int32, (tq, block), 1)
    peak = jnp.full((tq, 1), NEG_BIG, jnp.float32)
    denom = jnp.zeros((tq, 1), jnp.float32)
    accum = jnp.zeros((tq, HEAD_SIZE), jnp.float32)
    scale = HEAD_SIZE ** (-0.5)
    for j in range(n_blocks):
        kv = kv_refs[j]
        keys = kv[0, :, :HEAD_SIZE]
        values = kv[0, :, HEAD_SIZE:]
        scores = (
            lax.dot_general(
                q, keys, (((1,), (1,)), ((), ())), preferred_element_type=jnp.float32
            )
            * scale
        )
        t = j * block + col
        valid = t >= t0
        if j == 0:
            valid = valid & (t > row)
        if j == n_blocks - 1:
            valid = valid & (t <= row + WIN)
        peak_new = jnp.maximum(
            peak, jnp.max(jnp.where(valid, scores, NEG_BIG), axis=1, keepdims=True)
        )
        weights = jnp.where(valid, jnp.exp(scores - peak_new), 0.0)
        decay = jnp.exp(peak - peak_new)
        denom = denom * decay + jnp.sum(weights, axis=1, keepdims=True)
        accum = accum * decay + jnp.dot(
            weights.astype(jnp.bfloat16), values, preferred_element_type=jnp.float32
        )
        peak = peak_new
    o_ref[0] = (accum / denom).astype(o_ref.dtype)


def prefill_attention(pre_query, kv_blocks, first_key):
    local_pre, block_query, _ = pre_query.shape
    block = kv_blocks[0].shape[1]
    n_blocks = len(kv_blocks)
    tq = min(block_query, 512)
    kernel = functools.partial(prefill_kernel, n_blocks=n_blocks, block=block, tq=tq)
    kv_spec = pl.BlockSpec((1, block, 2 * HEAD_SIZE), lambda r, h, qi, t0: (r, 0, 0))
    q_spec = pl.BlockSpec((1, tq, HEAD_SIZE), lambda r, h, qi, t0: (r, qi, h))
    flops = 4 * local_pre * HQ * block_query * block * n_blocks * HEAD_SIZE
    return pl.pallas_call(
        kernel,
        out_shape=jax.ShapeDtypeStruct(pre_query.shape, jnp.bfloat16),
        grid_spec=pltpu.PrefetchScalarGridSpec(
            num_scalar_prefetch=1,
            grid=(local_pre, HQ, block_query // tq),
            in_specs=[q_spec] + [kv_spec] * n_blocks,
            out_specs=q_spec,
        ),
        compiler_params=pltpu.CompilerParams(
            dimension_semantics=("arbitrary", "arbitrary", "arbitrary")
        ),
        cost_estimate=pl.CostEstimate(
            flops=flops,
            transcendentals=local_pre * HQ * block_query * block * n_blocks,
            bytes_accessed=2 * pre_query.size * 2 + sum(b.size for b in kv_blocks) * 2,
        ),
    )(first_key, pre_query, *kv_blocks)


def body(
    pre_query,
    pre_fresh,
    pre_cache,
    pre_start,
    pre_resid,
    dec_query,
    dec_fresh,
    decode_window_cache,
    dec_length,
    dec_resid,
    out_weight,
    norm_gain,
    embedding,
):
    seq_count = lax.axis_size("seq")
    seq_index = lax.axis_index("seq")
    local_pre = pre_query.shape[0]
    block_query = pre_query.shape[1]
    score_scale = HEAD_SIZE ** (-0.5)
    kv_blocks = [None] * (seq_count + 1)
    kv_blocks[0] = pre_cache
    kv_blocks[seq_count] = pre_fresh
    for shift in range(1, seq_count):
        outgoing = jnp.where(seq_index + shift <= seq_count - 1, pre_fresh, pre_cache)
        kv_blocks[seq_count - shift] = from_behind(outgoing, "seq", shift)
    first_key = (WIN - seq_index * block_query - pre_start).astype(jnp.int32)
    pre_mixed_3d = prefill_attention(pre_query, kv_blocks, first_key)
    pre_mixed = pre_mixed_3d.reshape(local_pre * block_query, HQ * HEAD_SIZE)
    decode_token_rows = dec_query.reshape(-1, HQ, HEAD_SIZE)
    cache_scores = (
        jnp.einsum(
            "vfx,vzx->vfz",
            decode_token_rows,
            decode_window_cache[:, :, :HEAD_SIZE],
            preferred_element_type=jnp.float32,
        )
        * score_scale
    )
    self_scores = (
        jnp.einsum(
            "bhd,bd->bh",
            decode_token_rows,
            dec_fresh[:, :HEAD_SIZE],
            preferred_element_type=jnp.float32,
        )[:, :, None]
        * score_scale
    )
    slot_index = jnp.arange(WIN, dtype=jnp.int32)[None, :]
    length_col = dec_length[:, None]
    held_pos = length_col - 1 - jnp.mod(length_col - 1 - slot_index, WIN)
    live_mask = ((held_pos >= 0) & (held_pos > length_col - WIN))[:, None, :]
    peak_score = jnp.maximum(
        jnp.max(jnp.where(live_mask, cache_scores, NEG_BIG), axis=2, keepdims=True), self_scores
    )
    cache_attention_weights = jnp.where(live_mask, jnp.exp(cache_scores - peak_score), 0.0)
    self_weights = jnp.exp(self_scores - peak_score)
    denom_sum = jnp.sum(cache_attention_weights, axis=2, keepdims=True) + self_weights
    self_rounded = lax.optimization_barrier(self_weights.astype(jnp.bfloat16)).astype(jnp.float32)
    cache_part = jnp.einsum(
        "ect,ety->ecy",
        cache_attention_weights.astype(jnp.bfloat16),
        decode_window_cache[:, :, HEAD_SIZE:],
        preferred_element_type=jnp.float32,
    )
    self_part = self_rounded * dec_fresh[:, None, HEAD_SIZE:].astype(jnp.float32)
    dec_mixed = (
        ((cache_part + self_part) / denom_sum).astype(jnp.bfloat16).reshape(-1, HQ * HEAD_SIZE)
    )
    mixed_rows = jnp.concatenate([pre_mixed, dec_mixed], axis=0)
    projected = jnp.dot(
        mixed_rows,
        lax.all_gather(out_weight, "vocab", axis=0, tiled=True),
        preferred_element_type=jnp.float32,
    )
    pre_rows = local_pre * block_query
    pre_out = (
        pre_resid.astype(jnp.float32) + projected[:pre_rows].reshape(local_pre, block_query, D)
    ).astype(jnp.bfloat16)
    dec_out = (dec_resid.astype(jnp.float32) + projected[pre_rows:]).astype(jnp.bfloat16)
    local_dec = dec_mixed.shape[0]
    vocab_count = lax.axis_size("vocab")
    vocab_index = lax.axis_index("vocab")
    weight_rows = out_weight.shape[0]
    head_mixed = jnp.concatenate([dec_mixed, pre_mixed_3d[:, block_query - 1, :]], axis=0)
    head_resid = jnp.concatenate([dec_resid, pre_resid[:, block_query - 1, :]], axis=0)
    group_rows = lax.all_gather(
        jnp.concatenate([head_mixed, head_resid], axis=1), "vocab", axis=0, tiled=True
    )
    own_columns = lax.dynamic_slice_in_dim(
        group_rows, vocab_index * weight_rows, weight_rows, axis=1
    )
    partial = jnp.dot(own_columns, out_weight, preferred_element_type=jnp.float32)
    head_proj = lax.psum(partial, "vocab")
    head_in = (group_rows[:, D:].astype(jnp.float32) + head_proj).astype(jnp.bfloat16)
    everyone = lax.all_gather(normalize(head_in, norm_gain), "seq", axis=0, tiled=True)
    layout = everyone.reshape(seq_count, vocab_count, local_dec + local_pre, D)
    decode_all = layout[:, :, :local_dec].reshape(-1, D)
    prefill_every_request = layout[seq_count - 1, :, local_dec:].reshape(-1, D)
    head_rows = jnp.concatenate([decode_all, prefill_every_request], axis=0)
    logits = lax.dot_general(
        head_rows, embedding, (((1,), (1,)), ((), ())), preferred_element_type=jnp.float32
    )
    local_peak = jnp.max(logits, axis=1)
    local_sum = jnp.sum(jnp.exp(logits - local_peak[:, None]), axis=1)
    stats = gather_all(jnp.stack([local_peak, local_sum])[None])
    global_peak = jnp.max(stats[:, 0], axis=0)
    global_sum = jnp.sum(stats[:, 1] * jnp.exp(stats[:, 0] - global_peak[None]), axis=0)
    total = (global_peak + jnp.log(global_sum))[:, None]
    log_probs = (logits - total).astype(jnp.bfloat16)
    dec_count = decode_all.shape[0]
    return (pre_out, dec_out, log_probs[:dec_count], log_probs[dec_count:])


def solution(mesh):
    in_specs = (
        P("vocab", "seq", None),
        P("vocab", "seq", None),
        P("vocab", "seq", None),
        P("vocab"),
        P("vocab", "seq", None),
        P(("seq", "vocab"), None),
        P(("seq", "vocab"), None),
        P(("seq", "vocab"), None, None),
        P(("seq", "vocab")),
        P(("seq", "vocab"), None),
        P("vocab", None),
        P(),
        P(("seq", "vocab"), None),
    )
    out_specs = (
        P("vocab", "seq", None),
        P(("seq", "vocab"), None),
        P(None, ("seq", "vocab")),
        P(None, ("seq", "vocab")),
    )
    return jax.shard_map(body, mesh=mesh, in_specs=in_specs, out_specs=out_specs, check_vma=False)
```

```python
import functools

import jax
import jax.numpy as jnp
from jax import lax
from jax.experimental import pallas as pl
from jax.experimental.pallas import tpu as pltpu
from jax.sharding import PartitionSpec as P

D = 2560
HQ = 10
HEAD_SIZE = 256
WIN = 2048


NEG_BIG = -1e30
STABILITY_FLOOR = 1e-06


def from_behind(value, axis, steps):
    count = lax.axis_size(axis)
    pairs = [(source, (source + steps) % count) for source in range(count)]
    return lax.ppermute(value, axis, pairs)


def gather_all(value):
    inner = lax.all_gather(value, "vocab", axis=0, tiled=True)
    return lax.all_gather(inner, "seq", axis=0, tiled=True)


def normalize(rows_in, gain):
    values = rows_in.astype(jnp.float32)
    square_mean = jnp.mean(values * values, axis=-1, keepdims=True)
    return (values * lax.rsqrt(square_mean + STABILITY_FLOOR) * gain).astype(jnp.bfloat16)


def prefill_kernel(t0_ref, q_ref, *refs, n_blocks, block, tq):
    kv_refs = refs[:n_blocks]
    o_ref = refs[n_blocks]
    r = pl.program_id(0)
    qi = pl.program_id(2)
    t0 = t0_ref[r]
    q = q_ref[0]
    row = qi * tq + lax.broadcasted_iota(jnp.int32, (tq, block), 0)
    col = lax.broadcasted_iota(jnp.int32, (tq, block), 1)
    peak = jnp.full((tq, 1), NEG_BIG, jnp.float32)
    denom = jnp.zeros((tq, 1), jnp.float32)
    accum = jnp.zeros((tq, HEAD_SIZE), jnp.float32)
    scale = HEAD_SIZE ** (-0.5)
    for j in range(n_blocks):
        kv = kv_refs[j]
        keys = kv[0, :, :HEAD_SIZE]
        values = kv[0, :, HEAD_SIZE:]
        scores = (
            lax.dot_general(
                q, keys, (((1,), (1,)), ((), ())), preferred_element_type=jnp.float32
            )
            * scale
        )
        t = j * block + col
        valid = t >= t0
        if j == 0:
            valid = valid & (t > row)
        if j == n_blocks - 1:
            valid = valid & (t <= row + WIN)
        peak_new = jnp.maximum(
            peak, jnp.max(jnp.where(valid, scores, NEG_BIG), axis=1, keepdims=True)
        )
        weights = jnp.where(valid, jnp.exp(scores - peak_new), 0.0)
        decay = jnp.exp(peak - peak_new)
        denom = denom * decay + jnp.sum(weights, axis=1, keepdims=True)
        accum = accum * decay + jnp.dot(
            weights.astype(jnp.bfloat16), values, preferred_element_type=jnp.float32
        )
        peak = peak_new
    o_ref[0] = (accum / denom).astype(o_ref.dtype)


def prefill_attention(pre_query, kv_blocks, first_key):
    local_pre, block_query, _ = pre_query.shape
    block = kv_blocks[0].shape[1]
    n_blocks = len(kv_blocks)
    tq = min(block_query, 512)
    kernel = functools.partial(prefill_kernel, n_blocks=n_blocks, block=block, tq=tq)
    kv_spec = pl.BlockSpec((1, block, 2 * HEAD_SIZE), lambda r, h, qi, t0: (r, 0, 0))
    q_spec = pl.BlockSpec((1, tq, HEAD_SIZE), lambda r, h, qi, t0: (r, qi, h))
    flops = 4 * local_pre * HQ * block_query * block * n_blocks * HEAD_SIZE
    return pl.pallas_call(
        kernel,
        out_shape=jax.ShapeDtypeStruct(pre_query.shape, jnp.bfloat16),
        grid_spec=pltpu.PrefetchScalarGridSpec(
            num_scalar_prefetch=1,
            grid=(local_pre, HQ, block_query // tq),
            in_specs=[q_spec] + [kv_spec] * n_blocks,
            out_specs=q_spec,
        ),
        compiler_params=pltpu.CompilerParams(
            dimension_semantics=("arbitrary", "arbitrary", "arbitrary")
        ),
        cost_estimate=pl.CostEstimate(
            flops=flops,
            transcendentals=local_pre * HQ * block_query * block * n_blocks,
            bytes_accessed=2 * pre_query.size * 2 + sum(b.size for b in kv_blocks) * 2,
        ),
    )(first_key, pre_query, *kv_blocks)


def body(
    pre_query,
    pre_fresh,
    pre_cache,
    pre_start,
    pre_resid,
    dec_query,
    dec_fresh,
    decode_window_cache,
    dec_length,
    dec_resid,
    out_weight,
    norm_gain,
    embedding,
):
    seq_count = lax.axis_size("seq")
    seq_index = lax.axis_index("seq")
    local_pre = pre_query.shape[0]
    block_query = pre_query.shape[1]
    score_scale = HEAD_SIZE ** (-0.5)
    kv_blocks = [None] * (seq_count + 1)
    kv_blocks[0] = pre_cache
    kv_blocks[seq_count] = pre_fresh
    for shift in range(1, seq_count):
        outgoing = jnp.where(seq_index + shift <= seq_count - 1, pre_fresh, pre_cache)
        kv_blocks[seq_count - shift] = from_behind(outgoing, "seq", shift)
    first_key = (WIN - seq_index * block_query - pre_start).astype(jnp.int32)
    pre_mixed_3d = prefill_attention(pre_query, kv_blocks, first_key)
    pre_mixed = pre_mixed_3d.reshape(local_pre * block_query, HQ * HEAD_SIZE)
    decode_token_rows = dec_query.reshape(-1, HQ, HEAD_SIZE)
    cache_scores = (
        jnp.einsum(
            "vfx,vzx->vfz",
            decode_token_rows,
            decode_window_cache[:, :, :HEAD_SIZE],
            preferred_element_type=jnp.float32,
        )
        * score_scale
    )
    self_scores = (
        jnp.einsum(
            "bhd,bd->bh",
            decode_token_rows,
            dec_fresh[:, :HEAD_SIZE],
            preferred_element_type=jnp.float32,
        )[:, :, None]
        * score_scale
    )
    slot_index = jnp.arange(WIN, dtype=jnp.int32)[None, :]
    length_col = dec_length[:, None]
    held_pos = length_col - 1 - jnp.mod(length_col - 1 - slot_index, WIN)
    live_mask = ((held_pos >= 0) & (held_pos > length_col - WIN))[:, None, :]
    peak_score = jnp.maximum(
        jnp.max(jnp.where(live_mask, cache_scores, NEG_BIG), axis=2, keepdims=True), self_scores
    )
    cache_attention_weights = jnp.where(live_mask, jnp.exp(cache_scores - peak_score), 0.0)
    self_weights = jnp.exp(self_scores - peak_score)
    denom_sum = jnp.sum(cache_attention_weights, axis=2, keepdims=True) + self_weights
    self_rounded = lax.optimization_barrier(self_weights.astype(jnp.bfloat16)).astype(jnp.float32)
    cache_part = jnp.einsum(
        "ect,ety->ecy",
        cache_attention_weights.astype(jnp.bfloat16),
        decode_window_cache[:, :, HEAD_SIZE:],
        preferred_element_type=jnp.float32,
    )
    self_part = self_rounded * dec_fresh[:, None, HEAD_SIZE:].astype(jnp.float32)
    dec_mixed = (
        ((cache_part + self_part) / denom_sum).astype(jnp.bfloat16).reshape(-1, HQ * HEAD_SIZE)
    )
    mixed_rows = jnp.concatenate([pre_mixed, dec_mixed], axis=0)
    projected = jnp.dot(
        mixed_rows,
        lax.all_gather(out_weight, "vocab", axis=0, tiled=True),
        preferred_element_type=jnp.float32,
    )
    pre_rows = local_pre * block_query
    pre_out = (
        pre_resid.astype(jnp.float32) + projected[:pre_rows].reshape(local_pre, block_query, D)
    ).astype(jnp.bfloat16)
    dec_out = (dec_resid.astype(jnp.float32) + projected[pre_rows:]).astype(jnp.bfloat16)
    local_dec = dec_mixed.shape[0]
    vocab_count = lax.axis_size("vocab")
    vocab_index = lax.axis_index("vocab")
    weight_rows = out_weight.shape[0]
    head_count = local_dec + local_pre
    head_mixed = jnp.concatenate([dec_mixed, pre_mixed_3d[:, block_query - 1, :]], axis=0)
    head_resid = jnp.concatenate([dec_resid, pre_resid[:, block_query - 1, :]], axis=0)
    group_rows = lax.all_gather(head_mixed, "vocab", axis=0, tiled=True)
    own_columns = lax.dynamic_slice_in_dim(
        group_rows, vocab_index * weight_rows, weight_rows, axis=1
    )
    partial = jnp.dot(own_columns, out_weight, preferred_element_type=jnp.float32)
    pieces = lax.all_to_all(
        partial.reshape(vocab_count, head_count, D), "vocab", 0, 0, tiled=True
    )
    head_proj = jnp.sum(pieces, axis=0)
    head_in = (head_resid.astype(jnp.float32) + head_proj).astype(jnp.bfloat16)
    everyone = gather_all(normalize(head_in, norm_gain))
    layout = everyone.reshape(seq_count, vocab_count, head_count, D)
    decode_all = layout[:, :, :local_dec].reshape(-1, D)
    prefill_every_request = layout[seq_count - 1, :, local_dec:].reshape(-1, D)
    head_rows = jnp.concatenate([decode_all, prefill_every_request], axis=0)
    logits = lax.dot_general(
        head_rows, embedding, (((1,), (1,)), ((), ())), preferred_element_type=jnp.float32
    )
    local_peak = jnp.max(logits, axis=1)
    local_sum = jnp.sum(jnp.exp(logits - local_peak[:, None]), axis=1)
    stats = gather_all(jnp.stack([local_peak, local_sum])[None])
    global_peak = jnp.max(stats[:, 0], axis=0)
    global_sum = jnp.sum(stats[:, 1] * jnp.exp(stats[:, 0] - global_peak[None]), axis=0)
    total = (global_peak + jnp.log(global_sum))[:, None]
    log_probs = (logits - total).astype(jnp.bfloat16)
    dec_count = decode_all.shape[0]
    return (pre_out, dec_out, log_probs[:dec_count], log_probs[dec_count:])


def solution(mesh):
    in_specs = (
        P("vocab", "seq", None),
        P("vocab", "seq", None),
        P("vocab", "seq", None),
        P("vocab"),
        P("vocab", "seq", None),
        P(("seq", "vocab"), None),
        P(("seq", "vocab"), None),
        P(("seq", "vocab"), None, None),
        P(("seq", "vocab")),
        P(("seq", "vocab"), None),
        P("vocab", None),
        P(),
        P(("seq", "vocab"), None),
    )
    out_specs = (
        P("vocab", "seq", None),
        P(("seq", "vocab"), None),
        P(None, ("seq", "vocab")),
        P(None, ("seq", "vocab")),
    )
    return jax.shard_map(body, mesh=mesh, in_specs=in_specs, out_specs=out_specs, check_vma=False)
```

```python
import functools

import jax
import jax.numpy as jnp
from jax import lax
from jax.experimental import pallas as pl
from jax.experimental.pallas import tpu as pltpu
from jax.sharding import PartitionSpec as P

D = 2560
HQ = 10
HEAD_SIZE = 256
WIN = 2048


NEG_BIG = -1e30
STABILITY_FLOOR = 1e-06


def from_behind(value, axis, steps):
    count = lax.axis_size(axis)
    pairs = [(source, (source + steps) % count) for source in range(count)]
    return lax.ppermute(value, axis, pairs)


def gather_all(value):
    inner = lax.all_gather(value, "vocab", axis=0, tiled=True)
    return lax.all_gather(inner, "seq", axis=0, tiled=True)


def pairwise_sum(value, axis):
    count = lax.axis_size(axis)
    if count & (count - 1):
        return lax.psum(value, axis)
    step = 1
    while step < count:
        pairs = [(source, source ^ step) for source in range(count)]
        value = value + lax.ppermute(value, axis, pairs)
        step *= 2
    return value


def normalize(rows_in, gain):
    values = rows_in.astype(jnp.float32)
    square_mean = jnp.mean(values * values, axis=-1, keepdims=True)
    return (values * lax.rsqrt(square_mean + STABILITY_FLOOR) * gain).astype(jnp.bfloat16)


def prefill_kernel(t0_ref, q_ref, *refs, n_blocks, block, tq):
    kv_refs = refs[:n_blocks]
    o_ref = refs[n_blocks]
    r = pl.program_id(0)
    qi = pl.program_id(2)
    t0 = t0_ref[r]
    q = q_ref[0]
    row = qi * tq + lax.broadcasted_iota(jnp.int32, (tq, block), 0)
    col = lax.broadcasted_iota(jnp.int32, (tq, block), 1)
    peak = jnp.full((tq, 1), NEG_BIG, jnp.float32)
    denom = jnp.zeros((tq, 1), jnp.float32)
    accum = jnp.zeros((tq, HEAD_SIZE), jnp.float32)
    scale = HEAD_SIZE ** (-0.5)
    for j in range(n_blocks):
        kv = kv_refs[j]
        keys = kv[0, :, :HEAD_SIZE]
        values = kv[0, :, HEAD_SIZE:]
        scores = (
            lax.dot_general(
                q, keys, (((1,), (1,)), ((), ())), preferred_element_type=jnp.float32
            )
            * scale
        )
        t = j * block + col
        valid = t >= t0
        if j == 0:
            valid = valid & (t > row)
        if j == n_blocks - 1:
            valid = valid & (t <= row + WIN)
        peak_new = jnp.maximum(
            peak, jnp.max(jnp.where(valid, scores, NEG_BIG), axis=1, keepdims=True)
        )
        weights = jnp.where(valid, jnp.exp(scores - peak_new), 0.0)
        decay = jnp.exp(peak - peak_new)
        denom = denom * decay + jnp.sum(weights, axis=1, keepdims=True)
        accum = accum * decay + jnp.dot(
            weights.astype(jnp.bfloat16), values, preferred_element_type=jnp.float32
        )
        peak = peak_new
    o_ref[0] = (accum / denom).astype(o_ref.dtype)


def prefill_attention(pre_query, kv_blocks, first_key):
    local_pre, block_query, _ = pre_query.shape
    block = kv_blocks[0].shape[1]
    n_blocks = len(kv_blocks)
    tq = min(block_query, 512)
    kernel = functools.partial(prefill_kernel, n_blocks=n_blocks, block=block, tq=tq)
    kv_spec = pl.BlockSpec((1, block, 2 * HEAD_SIZE), lambda r, h, qi, t0: (r, 0, 0))
    q_spec = pl.BlockSpec((1, tq, HEAD_SIZE), lambda r, h, qi, t0: (r, qi, h))
    flops = 4 * local_pre * HQ * block_query * block * n_blocks * HEAD_SIZE
    return pl.pallas_call(
        kernel,
        out_shape=jax.ShapeDtypeStruct(pre_query.shape, jnp.bfloat16),
        grid_spec=pltpu.PrefetchScalarGridSpec(
            num_scalar_prefetch=1,
            grid=(local_pre, HQ, block_query // tq),
            in_specs=[q_spec] + [kv_spec] * n_blocks,
            out_specs=q_spec,
        ),
        compiler_params=pltpu.CompilerParams(
            dimension_semantics=("arbitrary", "arbitrary", "arbitrary")
        ),
        cost_estimate=pl.CostEstimate(
            flops=flops,
            transcendentals=local_pre * HQ * block_query * block * n_blocks,
            bytes_accessed=2 * pre_query.size * 2 + sum(b.size for b in kv_blocks) * 2,
        ),
    )(first_key, pre_query, *kv_blocks)


def body(
    pre_query,
    pre_fresh,
    pre_cache,
    pre_start,
    pre_resid,
    dec_query,
    dec_fresh,
    decode_window_cache,
    dec_length,
    dec_resid,
    out_weight,
    norm_gain,
    embedding,
):
    seq_count = lax.axis_size("seq")
    seq_index = lax.axis_index("seq")
    local_pre = pre_query.shape[0]
    block_query = pre_query.shape[1]
    score_scale = HEAD_SIZE ** (-0.5)
    kv_blocks = [None] * (seq_count + 1)
    kv_blocks[0] = pre_cache
    kv_blocks[seq_count] = pre_fresh
    for shift in range(1, seq_count):
        outgoing = jnp.where(seq_index + shift <= seq_count - 1, pre_fresh, pre_cache)
        kv_blocks[seq_count - shift] = from_behind(outgoing, "seq", shift)
    first_key = (WIN - seq_index * block_query - pre_start).astype(jnp.int32)
    pre_mixed_3d = prefill_attention(pre_query, kv_blocks, first_key)
    pre_mixed = pre_mixed_3d.reshape(local_pre * block_query, HQ * HEAD_SIZE)
    decode_token_rows = dec_query.reshape(-1, HQ, HEAD_SIZE)
    cache_scores = (
        jnp.einsum(
            "vfx,vzx->vfz",
            decode_token_rows,
            decode_window_cache[:, :, :HEAD_SIZE],
            preferred_element_type=jnp.float32,
        )
        * score_scale
    )
    self_scores = (
        jnp.einsum(
            "bhd,bd->bh",
            decode_token_rows,
            dec_fresh[:, :HEAD_SIZE],
            preferred_element_type=jnp.float32,
        )[:, :, None]
        * score_scale
    )
    slot_index = jnp.arange(WIN, dtype=jnp.int32)[None, :]
    length_col = dec_length[:, None]
    held_pos = length_col - 1 - jnp.mod(length_col - 1 - slot_index, WIN)
    live_mask = ((held_pos >= 0) & (held_pos > length_col - WIN))[:, None, :]
    peak_score = jnp.maximum(
        jnp.max(jnp.where(live_mask, cache_scores, NEG_BIG), axis=2, keepdims=True), self_scores
    )
    cache_attention_weights = jnp.where(live_mask, jnp.exp(cache_scores - peak_score), 0.0)
    self_weights = jnp.exp(self_scores - peak_score)
    denom_sum = jnp.sum(cache_attention_weights, axis=2, keepdims=True) + self_weights
    self_rounded = lax.optimization_barrier(self_weights.astype(jnp.bfloat16)).astype(jnp.float32)
    cache_part = jnp.einsum(
        "ect,ety->ecy",
        cache_attention_weights.astype(jnp.bfloat16),
        decode_window_cache[:, :, HEAD_SIZE:],
        preferred_element_type=jnp.float32,
    )
    self_part = self_rounded * dec_fresh[:, None, HEAD_SIZE:].astype(jnp.float32)
    dec_mixed = (
        ((cache_part + self_part) / denom_sum).astype(jnp.bfloat16).reshape(-1, HQ * HEAD_SIZE)
    )
    mixed_rows = jnp.concatenate([pre_mixed, dec_mixed], axis=0)
    projected = jnp.dot(
        mixed_rows,
        lax.all_gather(out_weight, "vocab", axis=0, tiled=True),
        preferred_element_type=jnp.float32,
    )
    pre_rows = local_pre * block_query
    pre_out = (
        pre_resid.astype(jnp.float32) + projected[:pre_rows].reshape(local_pre, block_query, D)
    ).astype(jnp.bfloat16)
    dec_out = (dec_resid.astype(jnp.float32) + projected[pre_rows:]).astype(jnp.bfloat16)
    local_dec = dec_mixed.shape[0]
    vocab_count = lax.axis_size("vocab")
    vocab_index = lax.axis_index("vocab")
    weight_rows = out_weight.shape[0]
    head_count = local_dec + local_pre
    head_mixed = jnp.concatenate([dec_mixed, pre_mixed_3d[:, block_query - 1, :]], axis=0)
    head_resid = jnp.concatenate([dec_resid, pre_resid[:, block_query - 1, :]], axis=0)
    group_rows = lax.all_gather(
        jnp.concatenate([head_mixed, head_resid], axis=1), "vocab", axis=0, tiled=True
    )
    own_columns = lax.dynamic_slice_in_dim(
        group_rows, vocab_index * weight_rows, weight_rows, axis=1
    )
    partial = jnp.dot(own_columns, out_weight, preferred_element_type=jnp.float32)
    head_proj = pairwise_sum(partial, "vocab")
    head_in = (group_rows[:, D:].astype(jnp.float32) + head_proj).astype(jnp.bfloat16)
    everyone = lax.all_gather(normalize(head_in, norm_gain), "seq", axis=0, tiled=True)
    layout = everyone.reshape(seq_count, vocab_count, head_count, D)
    decode_all = layout[:, :, :local_dec].reshape(-1, D)
    prefill_every_request = layout[seq_count - 1, :, local_dec:].reshape(-1, D)
    head_rows = jnp.concatenate([decode_all, prefill_every_request], axis=0)
    logits = lax.dot_general(
        head_rows, embedding, (((1,), (1,)), ((), ())), preferred_element_type=jnp.float32
    )
    local_peak = jnp.max(logits, axis=1)
    local_sum = jnp.sum(jnp.exp(logits - local_peak[:, None]), axis=1)
    stats = gather_all(jnp.stack([local_peak, local_sum])[None])
    global_peak = jnp.max(stats[:, 0], axis=0)
    global_sum = jnp.sum(stats[:, 1] * jnp.exp(stats[:, 0] - global_peak[None]), axis=0)
    total = (global_peak + jnp.log(global_sum))[:, None]
    log_probs = (logits - total).astype(jnp.bfloat16)
    dec_count = decode_all.shape[0]
    return (pre_out, dec_out, log_probs[:dec_count], log_probs[dec_count:])


def solution(mesh):
    in_specs = (
        P("vocab", "seq", None),
        P("vocab", "seq", None),
        P("vocab", "seq", None),
        P("vocab"),
        P("vocab", "seq", None),
        P(("seq", "vocab"), None),
        P(("seq", "vocab"), None),
        P(("seq", "vocab"), None, None),
        P(("seq", "vocab")),
        P(("seq", "vocab"), None),
        P("vocab", None),
        P(),
        P(("seq", "vocab"), None),
    )
    out_specs = (
        P("vocab", "seq", None),
        P(("seq", "vocab"), None),
        P(None, ("seq", "vocab")),
        P(None, ("seq", "vocab")),
    )
    return jax.shard_map(body, mesh=mesh, in_specs=in_specs, out_specs=out_specs, check_vma=False)
```

```python
import functools

import jax
import jax.numpy as jnp
from jax import lax
from jax.experimental import pallas as pl
from jax.experimental.pallas import tpu as pltpu
from jax.sharding import PartitionSpec as P

D = 2560
HQ = 10
HEAD_SIZE = 256
WIN = 2048


NEG_BIG = -1e30
STABILITY_FLOOR = 1e-06


def from_behind(value, axis, steps):
    count = lax.axis_size(axis)
    pairs = [(source, (source + steps) % count) for source in range(count)]
    return lax.ppermute(value, axis, pairs)


def gather_all(value):
    inner = lax.all_gather(value, "vocab", axis=0, tiled=True)
    return lax.all_gather(inner, "seq", axis=0, tiled=True)


def normalize(rows_in, gain):
    values = rows_in.astype(jnp.float32)
    square_mean = jnp.mean(values * values, axis=-1, keepdims=True)
    return (values * lax.rsqrt(square_mean + STABILITY_FLOOR) * gain).astype(jnp.bfloat16)


def prefill_kernel(t0_ref, q_ref, *refs, positions, n_blocks, block, tq, carry_in, final):
    n_in = len(positions)
    if carry_in:
        peak_ref, denom_ref, accum_ref = refs[:3]
        refs = refs[3:]
    kv_refs = refs[:n_in]
    out_refs = refs[n_in:]
    r = pl.program_id(0)
    qi = pl.program_id(2)
    t0 = t0_ref[r]
    q = q_ref[0]
    row = qi * tq + lax.broadcasted_iota(jnp.int32, (tq, block), 0)
    col = lax.broadcasted_iota(jnp.int32, (tq, block), 1)
    if carry_in:
        state = (peak_ref[0, 0], denom_ref[0, 0], accum_ref[0])
    else:
        state = (
            jnp.full((tq, 1), NEG_BIG, jnp.float32),
            jnp.zeros((tq, 1), jnp.float32),
            jnp.zeros((tq, HEAD_SIZE), jnp.float32),
        )
    scale = HEAD_SIZE ** (-0.5)
    for kv, j in zip(kv_refs, positions):
        keys = kv[0, :, :HEAD_SIZE]
        values = kv[0, :, HEAD_SIZE:]

        def absorb(state, valid):
            peak, denom, accum = state
            scores = (
                lax.dot_general(
                    q, keys, (((1,), (1,)), ((), ())), preferred_element_type=jnp.float32
                )
                * scale
            )
            if valid is None:
                peak_new = jnp.maximum(peak, jnp.max(scores, axis=1, keepdims=True))
                weights = jnp.exp(scores - peak_new)
            else:
                peak_new = jnp.maximum(
                    peak, jnp.max(jnp.where(valid, scores, NEG_BIG), axis=1, keepdims=True)
                )
                weights = jnp.where(valid, jnp.exp(scores - peak_new), 0.0)
            decay = jnp.exp(peak - peak_new)
            denom = denom * decay + jnp.sum(weights, axis=1, keepdims=True)
            accum = accum * decay + jnp.dot(
                weights.astype(jnp.bfloat16), values, preferred_element_type=jnp.float32
            )
            return (peak_new, denom, accum)

        def masked(state):
            t = j * block + col
            valid = t >= t0
            if j == 0:
                valid = valid & (t > row)
            if j == n_blocks - 1:
                valid = valid & (t <= row + WIN)
            return absorb(state, valid)

        if j == 0 or j == n_blocks - 1:
            state = masked(state)
        else:
            state = lax.cond(
                t0 <= j * block, lambda st: absorb(st, None), masked, state
            )
    peak, denom, accum = state
    if final:
        out_refs[0][0] = (accum / denom).astype(out_refs[0].dtype)
    else:
        out_refs[0][0, 0] = peak
        out_refs[1][0, 0] = denom
        out_refs[2][0] = accum


def prefill_pass(pre_query, kv_blocks, positions, n_blocks, first_key, carry, final):
    local_pre, block_query, _ = pre_query.shape
    block = kv_blocks[0].shape[1]
    tq = min(block_query, 512)
    kernel = functools.partial(
        prefill_kernel,
        positions=tuple(positions),
        n_blocks=n_blocks,
        block=block,
        tq=tq,
        carry_in=carry is not None,
        final=final,
    )
    kv_spec = pl.BlockSpec((1, block, 2 * HEAD_SIZE), lambda r, h, qi, t0: (r, 0, 0))
    q_spec = pl.BlockSpec((1, tq, HEAD_SIZE), lambda r, h, qi, t0: (r, qi, h))
    stat_spec = pl.BlockSpec((1, 1, tq, 1), lambda r, h, qi, t0: (r, h, qi, 0))
    stat_shape = jax.ShapeDtypeStruct((local_pre, HQ, block_query, 1), jnp.float32)
    accum_shape = jax.ShapeDtypeStruct(pre_query.shape, jnp.float32)
    carry_specs = [] if carry is None else [stat_spec, stat_spec, q_spec]
    carry_args = [] if carry is None else list(carry)
    if final:
        out_shape = jax.ShapeDtypeStruct(pre_query.shape, jnp.bfloat16)
        out_specs = q_spec
    else:
        out_shape = (stat_shape, stat_shape, accum_shape)
        out_specs = (stat_spec, stat_spec, q_spec)
    n_in = len(kv_blocks)
    flops = 4 * local_pre * HQ * block_query * block * n_in * HEAD_SIZE
    return pl.pallas_call(
        kernel,
        out_shape=out_shape,
        grid_spec=pltpu.PrefetchScalarGridSpec(
            num_scalar_prefetch=1,
            grid=(local_pre, HQ, block_query // tq),
            in_specs=[q_spec] + carry_specs + [kv_spec] * n_in,
            out_specs=out_specs,
        ),
        compiler_params=pltpu.CompilerParams(
            dimension_semantics=("arbitrary", "arbitrary", "arbitrary")
        ),
        cost_estimate=pl.CostEstimate(
            flops=flops,
            transcendentals=local_pre * HQ * block_query * block * n_in,
            bytes_accessed=2 * pre_query.size * 2 + sum(b.size for b in kv_blocks) * 2,
        ),
    )(first_key, pre_query, *carry_args, *kv_blocks)


def prefill_attention(pre_query, kv_blocks, first_key):
    n_blocks = len(kv_blocks)
    carry = prefill_pass(
        pre_query, [kv_blocks[0], kv_blocks[-1]], [0, n_blocks - 1], n_blocks,
        first_key, None, False,
    )
    middle = list(range(1, n_blocks - 1))
    return prefill_pass(
        pre_query, [kv_blocks[j] for j in middle], middle, n_blocks, first_key, carry, True
    )


def body(
    pre_query,
    pre_fresh,
    pre_cache,
    pre_start,
    pre_resid,
    dec_query,
    dec_fresh,
    decode_window_cache,
    dec_length,
    dec_resid,
    out_weight,
    norm_gain,
    embedding,
):
    seq_count = lax.axis_size("seq")
    seq_index = lax.axis_index("seq")
    local_pre = pre_query.shape[0]
    block_query = pre_query.shape[1]
    score_scale = HEAD_SIZE ** (-0.5)
    kv_blocks = [None] * (seq_count + 1)
    kv_blocks[0] = pre_cache
    kv_blocks[seq_count] = pre_fresh
    for shift in range(1, seq_count):
        outgoing = jnp.where(seq_index + shift <= seq_count - 1, pre_fresh, pre_cache)
        kv_blocks[seq_count - shift] = from_behind(outgoing, "seq", shift)
    first_key = (WIN - seq_index * block_query - pre_start).astype(jnp.int32)
    pre_mixed_3d = prefill_attention(pre_query, kv_blocks, first_key)
    pre_mixed = pre_mixed_3d.reshape(local_pre * block_query, HQ * HEAD_SIZE)
    decode_token_rows = dec_query.reshape(-1, HQ, HEAD_SIZE)
    cache_scores = (
        jnp.einsum(
            "vfx,vzx->vfz",
            decode_token_rows,
            decode_window_cache[:, :, :HEAD_SIZE],
            preferred_element_type=jnp.float32,
        )
        * score_scale
    )
    self_scores = (
        jnp.einsum(
            "bhd,bd->bh",
            decode_token_rows,
            dec_fresh[:, :HEAD_SIZE],
            preferred_element_type=jnp.float32,
        )[:, :, None]
        * score_scale
    )
    slot_index = jnp.arange(WIN, dtype=jnp.int32)[None, :]
    length_col = dec_length[:, None]
    held_pos = length_col - 1 - jnp.mod(length_col - 1 - slot_index, WIN)
    live_mask = ((held_pos >= 0) & (held_pos > length_col - WIN))[:, None, :]
    peak_score = jnp.maximum(
        jnp.max(jnp.where(live_mask, cache_scores, NEG_BIG), axis=2, keepdims=True), self_scores
    )
    cache_attention_weights = jnp.where(live_mask, jnp.exp(cache_scores - peak_score), 0.0)
    self_weights = jnp.exp(self_scores - peak_score)
    denom_sum = jnp.sum(cache_attention_weights, axis=2, keepdims=True) + self_weights
    self_rounded = lax.optimization_barrier(self_weights.astype(jnp.bfloat16)).astype(jnp.float32)
    cache_part = jnp.einsum(
        "ect,ety->ecy",
        cache_attention_weights.astype(jnp.bfloat16),
        decode_window_cache[:, :, HEAD_SIZE:],
        preferred_element_type=jnp.float32,
    )
    self_part = self_rounded * dec_fresh[:, None, HEAD_SIZE:].astype(jnp.float32)
    dec_mixed = (
        ((cache_part + self_part) / denom_sum).astype(jnp.bfloat16).reshape(-1, HQ * HEAD_SIZE)
    )
    mixed_rows = jnp.concatenate([pre_mixed, dec_mixed], axis=0)
    projected = jnp.dot(
        mixed_rows,
        lax.all_gather(out_weight, "vocab", axis=0, tiled=True),
        preferred_element_type=jnp.float32,
    )
    pre_rows = local_pre * block_query
    pre_out = (
        pre_resid.astype(jnp.float32) + projected[:pre_rows].reshape(local_pre, block_query, D)
    ).astype(jnp.bfloat16)
    dec_out = (dec_resid.astype(jnp.float32) + projected[pre_rows:]).astype(jnp.bfloat16)
    local_dec = dec_mixed.shape[0]
    vocab_count = lax.axis_size("vocab")
    vocab_index = lax.axis_index("vocab")
    weight_rows = out_weight.shape[0]
    head_count = local_dec + local_pre
    head_mixed = jnp.concatenate([dec_mixed, pre_mixed_3d[:, block_query - 1, :]], axis=0)
    head_resid = jnp.concatenate([dec_resid, pre_resid[:, block_query - 1, :]], axis=0)
    group_rows = lax.all_gather(head_mixed, "vocab", axis=0, tiled=True)
    own_columns = lax.dynamic_slice_in_dim(
        group_rows, vocab_index * weight_rows, weight_rows, axis=1
    )
    partial = jnp.dot(own_columns, out_weight, preferred_element_type=jnp.float32)
    pieces = lax.all_to_all(
        partial.reshape(vocab_count, head_count, D), "vocab", 0, 0, tiled=True
    )
    head_proj = jnp.sum(pieces, axis=0)
    head_in = (head_resid.astype(jnp.float32) + head_proj).astype(jnp.bfloat16)
    everyone = gather_all(normalize(head_in, norm_gain))
    layout = everyone.reshape(seq_count, vocab_count, head_count, D)
    decode_all = layout[:, :, :local_dec].reshape(-1, D)
    prefill_every_request = layout[seq_count - 1, :, local_dec:].reshape(-1, D)
    head_rows = jnp.concatenate([decode_all, prefill_every_request], axis=0)
    logits = lax.dot_general(
        head_rows, embedding, (((1,), (1,)), ((), ())), preferred_element_type=jnp.float32
    )
    local_peak = jnp.max(logits, axis=1)
    local_sum = jnp.sum(jnp.exp(logits - local_peak[:, None]), axis=1)
    stats = gather_all(jnp.stack([local_peak, local_sum])[None])
    global_peak = jnp.max(stats[:, 0], axis=0)
    global_sum = jnp.sum(stats[:, 1] * jnp.exp(stats[:, 0] - global_peak[None]), axis=0)
    total = (global_peak + jnp.log(global_sum))[:, None]
    log_probs = (logits - total).astype(jnp.bfloat16)
    dec_count = decode_all.shape[0]
    return (pre_out, dec_out, log_probs[:dec_count], log_probs[dec_count:])


def solution(mesh):
    in_specs = (
        P("vocab", "seq", None),
        P("vocab", "seq", None),
        P("vocab", "seq", None),
        P("vocab"),
        P("vocab", "seq", None),
        P(("seq", "vocab"), None),
        P(("seq", "vocab"), None),
        P(("seq", "vocab"), None, None),
        P(("seq", "vocab")),
        P(("seq", "vocab"), None),
        P("vocab", None),
        P(),
        P(("seq", "vocab"), None),
    )
    out_specs = (
        P("vocab", "seq", None),
        P(("seq", "vocab"), None),
        P(None, ("seq", "vocab")),
        P(None, ("seq", "vocab")),
    )
    return jax.shard_map(body, mesh=mesh, in_specs=in_specs, out_specs=out_specs, check_vma=False)
```

```python
import functools

import jax
import jax.numpy as jnp
from jax import lax
from jax.experimental import pallas as pl
from jax.experimental.pallas import tpu as pltpu
from jax.sharding import PartitionSpec as P

D = 2560
HQ = 10
HEAD_SIZE = 256
WIN = 2048


NEG_BIG = -1e30
STABILITY_FLOOR = 1e-06


def from_behind(value, axis, steps):
    count = lax.axis_size(axis)
    pairs = [(source, (source + steps) % count) for source in range(count)]
    return lax.ppermute(value, axis, pairs)


def gather_all(value):
    inner = lax.all_gather(value, "vocab", axis=0, tiled=True)
    return lax.all_gather(inner, "seq", axis=0, tiled=True)


def normalize(rows_in, gain):
    values = rows_in.astype(jnp.float32)
    square_mean = jnp.mean(values * values, axis=-1, keepdims=True)
    return (values * lax.rsqrt(square_mean + STABILITY_FLOOR) * gain).astype(jnp.bfloat16)


def prefill_kernel(t0_ref, q_ref, *refs, positions, n_blocks, block, tq, carry_in, final):
    n_in = len(positions)
    if carry_in:
        peak_ref, denom_ref, accum_ref = refs[:3]
        refs = refs[3:]
    kv_refs = refs[:n_in]
    out_refs = refs[n_in:]
    r = pl.program_id(0)
    qi = pl.program_id(2)
    t0 = t0_ref[r]
    q = q_ref[0]
    row = qi * tq + lax.broadcasted_iota(jnp.int32, (tq, block), 0)
    col = lax.broadcasted_iota(jnp.int32, (tq, block), 1)
    if carry_in:
        state = (peak_ref[0, 0], denom_ref[0, 0], accum_ref[0])
    else:
        state = (
            jnp.full((tq, 1), NEG_BIG, jnp.float32),
            jnp.zeros((tq, 1), jnp.float32),
            jnp.zeros((tq, HEAD_SIZE), jnp.float32),
        )
    scale = HEAD_SIZE ** (-0.5)
    for kv, j in zip(kv_refs, positions):
        keys = kv[0, :, :HEAD_SIZE]
        values = kv[0, :, HEAD_SIZE:]

        def absorb(state, valid):
            peak, denom, accum = state
            scores = (
                lax.dot_general(
                    q, keys, (((1,), (1,)), ((), ())), preferred_element_type=jnp.float32
                )
                * scale
            )
            if valid is None:
                peak_new = jnp.maximum(peak, jnp.max(scores, axis=1, keepdims=True))
                weights = jnp.exp(scores - peak_new)
            else:
                peak_new = jnp.maximum(
                    peak, jnp.max(jnp.where(valid, scores, NEG_BIG), axis=1, keepdims=True)
                )
                weights = jnp.where(valid, jnp.exp(scores - peak_new), 0.0)
            decay = jnp.exp(peak - peak_new)
            denom = denom * decay + jnp.sum(weights, axis=1, keepdims=True)
            accum = accum * decay + jnp.dot(
                weights.astype(jnp.bfloat16), values, preferred_element_type=jnp.float32
            )
            return (peak_new, denom, accum)

        def masked(state):
            t = j * block + col
            valid = t >= t0
            if j == 0:
                valid = valid & (t > row)
            if j == n_blocks - 1:
                valid = valid & (t <= row + WIN)
            return absorb(state, valid)

        state = masked(state)
    peak, denom, accum = state
    if final:
        out_refs[0][0] = (accum / denom).astype(out_refs[0].dtype)
    else:
        out_refs[0][0, 0] = peak
        out_refs[1][0, 0] = denom
        out_refs[2][0] = accum


def prefill_pass(pre_query, kv_blocks, positions, n_blocks, first_key, carry, final):
    local_pre, block_query, _ = pre_query.shape
    block = kv_blocks[0].shape[1]
    tq = min(block_query, 512)
    kernel = functools.partial(
        prefill_kernel,
        positions=tuple(positions),
        n_blocks=n_blocks,
        block=block,
        tq=tq,
        carry_in=carry is not None,
        final=final,
    )
    kv_spec = pl.BlockSpec((1, block, 2 * HEAD_SIZE), lambda r, h, qi, t0: (r, 0, 0))
    q_spec = pl.BlockSpec((1, tq, HEAD_SIZE), lambda r, h, qi, t0: (r, qi, h))
    stat_spec = pl.BlockSpec((1, 1, tq, 1), lambda r, h, qi, t0: (r, h, qi, 0))
    stat_shape = jax.ShapeDtypeStruct((local_pre, HQ, block_query, 1), jnp.float32)
    accum_shape = jax.ShapeDtypeStruct(pre_query.shape, jnp.float32)
    carry_specs = [] if carry is None else [stat_spec, stat_spec, q_spec]
    carry_args = [] if carry is None else list(carry)
    if final:
        out_shape = jax.ShapeDtypeStruct(pre_query.shape, jnp.bfloat16)
        out_specs = q_spec
    else:
        out_shape = (stat_shape, stat_shape, accum_shape)
        out_specs = (stat_spec, stat_spec, q_spec)
    n_in = len(kv_blocks)
    flops = 4 * local_pre * HQ * block_query * block * n_in * HEAD_SIZE
    return pl.pallas_call(
        kernel,
        out_shape=out_shape,
        grid_spec=pltpu.PrefetchScalarGridSpec(
            num_scalar_prefetch=1,
            grid=(local_pre, HQ, block_query // tq),
            in_specs=[q_spec] + carry_specs + [kv_spec] * n_in,
            out_specs=out_specs,
        ),
        compiler_params=pltpu.CompilerParams(
            dimension_semantics=("arbitrary", "arbitrary", "arbitrary")
        ),
        cost_estimate=pl.CostEstimate(
            flops=flops,
            transcendentals=local_pre * HQ * block_query * block * n_in,
            bytes_accessed=2 * pre_query.size * 2 + sum(b.size for b in kv_blocks) * 2,
        ),
    )(first_key, pre_query, *carry_args, *kv_blocks)


def prefill_attention(pre_query, kv_blocks, first_key):
    n_blocks = len(kv_blocks)
    carry = prefill_pass(
        pre_query, [kv_blocks[0], kv_blocks[-1]], [0, n_blocks - 1], n_blocks,
        first_key, None, False,
    )
    middle = list(range(1, n_blocks - 1))
    return prefill_pass(
        pre_query, [kv_blocks[j] for j in middle], middle, n_blocks, first_key, carry, True
    )


def body(
    pre_query,
    pre_fresh,
    pre_cache,
    pre_start,
    pre_resid,
    dec_query,
    dec_fresh,
    decode_window_cache,
    dec_length,
    dec_resid,
    out_weight,
    norm_gain,
    embedding,
):
    seq_count = lax.axis_size("seq")
    seq_index = lax.axis_index("seq")
    local_pre = pre_query.shape[0]
    block_query = pre_query.shape[1]
    score_scale = HEAD_SIZE ** (-0.5)
    kv_blocks = [None] * (seq_count + 1)
    kv_blocks[0] = pre_cache
    kv_blocks[seq_count] = pre_fresh
    for shift in range(1, seq_count):
        outgoing = jnp.where(seq_index + shift <= seq_count - 1, pre_fresh, pre_cache)
        kv_blocks[seq_count - shift] = from_behind(outgoing, "seq", shift)
    first_key = (WIN - seq_index * block_query - pre_start).astype(jnp.int32)
    pre_mixed_3d = prefill_attention(pre_query, kv_blocks, first_key)
    pre_mixed = pre_mixed_3d.reshape(local_pre * block_query, HQ * HEAD_SIZE)
    decode_token_rows = dec_query.reshape(-1, HQ, HEAD_SIZE)
    cache_scores = (
        jnp.einsum(
            "vfx,vzx->vfz",
            decode_token_rows,
            decode_window_cache[:, :, :HEAD_SIZE],
            preferred_element_type=jnp.float32,
        )
        * score_scale
    )
    self_scores = (
        jnp.einsum(
            "bhd,bd->bh",
            decode_token_rows,
            dec_fresh[:, :HEAD_SIZE],
            preferred_element_type=jnp.float32,
        )[:, :, None]
        * score_scale
    )
    slot_index = jnp.arange(WIN, dtype=jnp.int32)[None, :]
    length_col = dec_length[:, None]
    held_pos = length_col - 1 - jnp.mod(length_col - 1 - slot_index, WIN)
    live_mask = ((held_pos >= 0) & (held_pos > length_col - WIN))[:, None, :]
    peak_score = jnp.maximum(
        jnp.max(jnp.where(live_mask, cache_scores, NEG_BIG), axis=2, keepdims=True), self_scores
    )
    cache_attention_weights = jnp.where(live_mask, jnp.exp(cache_scores - peak_score), 0.0)
    self_weights = jnp.exp(self_scores - peak_score)
    denom_sum = jnp.sum(cache_attention_weights, axis=2, keepdims=True) + self_weights
    self_rounded = lax.optimization_barrier(self_weights.astype(jnp.bfloat16)).astype(jnp.float32)
    cache_part = jnp.einsum(
        "ect,ety->ecy",
        cache_attention_weights.astype(jnp.bfloat16),
        decode_window_cache[:, :, HEAD_SIZE:],
        preferred_element_type=jnp.float32,
    )
    self_part = self_rounded * dec_fresh[:, None, HEAD_SIZE:].astype(jnp.float32)
    dec_mixed = (
        ((cache_part + self_part) / denom_sum).astype(jnp.bfloat16).reshape(-1, HQ * HEAD_SIZE)
    )
    mixed_rows = jnp.concatenate([pre_mixed, dec_mixed], axis=0)
    projected = jnp.dot(
        mixed_rows,
        lax.all_gather(out_weight, "vocab", axis=0, tiled=True),
        preferred_element_type=jnp.float32,
    )
    pre_rows = local_pre * block_query
    pre_out = (
        pre_resid.astype(jnp.float32) + projected[:pre_rows].reshape(local_pre, block_query, D)
    ).astype(jnp.bfloat16)
    dec_out = (dec_resid.astype(jnp.float32) + projected[pre_rows:]).astype(jnp.bfloat16)
    local_dec = dec_mixed.shape[0]
    vocab_count = lax.axis_size("vocab")
    vocab_index = lax.axis_index("vocab")
    weight_rows = out_weight.shape[0]
    head_count = local_dec + local_pre
    head_mixed = jnp.concatenate([dec_mixed, pre_mixed_3d[:, block_query - 1, :]], axis=0)
    head_resid = jnp.concatenate([dec_resid, pre_resid[:, block_query - 1, :]], axis=0)
    group_rows = lax.all_gather(head_mixed, "vocab", axis=0, tiled=True)
    own_columns = lax.dynamic_slice_in_dim(
        group_rows, vocab_index * weight_rows, weight_rows, axis=1
    )
    partial = jnp.dot(own_columns, out_weight, preferred_element_type=jnp.float32)
    pieces = lax.all_to_all(
        partial.reshape(vocab_count, head_count, D), "vocab", 0, 0, tiled=True
    )
    head_proj = jnp.sum(pieces, axis=0)
    head_in = (head_resid.astype(jnp.float32) + head_proj).astype(jnp.bfloat16)
    everyone = gather_all(normalize(head_in, norm_gain))
    layout = everyone.reshape(seq_count, vocab_count, head_count, D)
    decode_all = layout[:, :, :local_dec].reshape(-1, D)
    prefill_every_request = layout[seq_count - 1, :, local_dec:].reshape(-1, D)
    head_rows = jnp.concatenate([decode_all, prefill_every_request], axis=0)
    logits = lax.dot_general(
        head_rows, embedding, (((1,), (1,)), ((), ())), preferred_element_type=jnp.float32
    )
    local_peak = jnp.max(logits, axis=1)
    local_sum = jnp.sum(jnp.exp(logits - local_peak[:, None]), axis=1)
    stats = gather_all(jnp.stack([local_peak, local_sum])[None])
    global_peak = jnp.max(stats[:, 0], axis=0)
    global_sum = jnp.sum(stats[:, 1] * jnp.exp(stats[:, 0] - global_peak[None]), axis=0)
    total = (global_peak + jnp.log(global_sum))[:, None]
    log_probs = (logits - total).astype(jnp.bfloat16)
    dec_count = decode_all.shape[0]
    return (pre_out, dec_out, log_probs[:dec_count], log_probs[dec_count:])


def solution(mesh):
    in_specs = (
        P("vocab", "seq", None),
        P("vocab", "seq", None),
        P("vocab", "seq", None),
        P("vocab"),
        P("vocab", "seq", None),
        P(("seq", "vocab"), None),
        P(("seq", "vocab"), None),
        P(("seq", "vocab"), None, None),
        P(("seq", "vocab")),
        P(("seq", "vocab"), None),
        P("vocab", None),
        P(),
        P(("seq", "vocab"), None),
    )
    out_specs = (
        P("vocab", "seq", None),
        P(("seq", "vocab"), None),
        P(None, ("seq", "vocab")),
        P(None, ("seq", "vocab")),
    )
    return jax.shard_map(body, mesh=mesh, in_specs=in_specs, out_specs=out_specs, check_vma=False)
```

```python
import functools

import jax
import jax.numpy as jnp
from jax import lax
from jax.experimental import pallas as pl
from jax.experimental.pallas import tpu as pltpu
from jax.sharding import PartitionSpec as P

D = 2560
HQ = 10
HEAD_SIZE = 256
WIN = 2048


NEG_BIG = -1e30
STABILITY_FLOOR = 1e-06


def from_behind(value, axis, steps):
    count = lax.axis_size(axis)
    pairs = [(source, (source + steps) % count) for source in range(count)]
    return lax.ppermute(value, axis, pairs)


def gather_all(value):
    inner = lax.all_gather(value, "vocab", axis=0, tiled=True)
    return lax.all_gather(inner, "seq", axis=0, tiled=True)


def normalize(rows_in, gain):
    values = rows_in.astype(jnp.float32)
    square_mean = jnp.mean(values * values, axis=-1, keepdims=True)
    return (values * lax.rsqrt(square_mean + STABILITY_FLOOR) * gain).astype(jnp.bfloat16)


def prefill_kernel(t0_ref, q_ref, *refs, n_blocks, block, tq):
    kv_refs = refs[:n_blocks]
    o_ref = refs[n_blocks]
    r = pl.program_id(0)
    qi = pl.program_id(2)
    t0 = t0_ref[r]
    q = q_ref[0]
    row = qi * tq + lax.broadcasted_iota(jnp.int32, (tq, block), 0)
    col = lax.broadcasted_iota(jnp.int32, (tq, block), 1)
    peak = jnp.full((tq, 1), NEG_BIG, jnp.float32)
    denom = jnp.zeros((tq, 1), jnp.float32)
    accum = jnp.zeros((tq, HEAD_SIZE), jnp.float32)
    scale = HEAD_SIZE ** (-0.5)
    for j in range(n_blocks):
        kv = kv_refs[j]
        keys = kv[0, :, :HEAD_SIZE]
        values = kv[0, :, HEAD_SIZE:]
        scores = (
            lax.dot_general(
                q, keys, (((1,), (1,)), ((), ())), preferred_element_type=jnp.float32
            )
            * scale
        )
        t = j * block + col
        if j == 0 or j == n_blocks - 1:
            valid = t >= t0
            if j == 0:
                valid = valid & (t > row)
            else:
                valid = valid & (t <= row + WIN)
            scores = jnp.where(valid, scores, NEG_BIG)
        else:
            key = j * block + lax.broadcasted_iota(jnp.int32, (1, block), 1)
            scores = scores + jnp.where(key >= t0, 0.0, NEG_BIG)
        peak_new = jnp.maximum(peak, jnp.max(scores, axis=1, keepdims=True))
        weights = jnp.exp(scores - peak_new)
        decay = jnp.exp(peak - peak_new)
        denom = denom * decay + jnp.sum(weights, axis=1, keepdims=True)
        accum = accum * decay + jnp.dot(
            weights.astype(jnp.bfloat16), values, preferred_element_type=jnp.float32
        )
        peak = peak_new
    o_ref[0] = (accum / denom).astype(o_ref.dtype)


def prefill_attention(pre_query, kv_blocks, first_key):
    local_pre, block_query, _ = pre_query.shape
    block = kv_blocks[0].shape[1]
    n_blocks = len(kv_blocks)
    tq = min(block_query, 512)
    kernel = functools.partial(prefill_kernel, n_blocks=n_blocks, block=block, tq=tq)
    kv_spec = pl.BlockSpec((1, block, 2 * HEAD_SIZE), lambda r, h, qi, t0: (r, 0, 0))
    q_spec = pl.BlockSpec((1, tq, HEAD_SIZE), lambda r, h, qi, t0: (r, qi, h))
    flops = 4 * local_pre * HQ * block_query * block * n_blocks * HEAD_SIZE
    return pl.pallas_call(
        kernel,
        out_shape=jax.ShapeDtypeStruct(pre_query.shape, jnp.bfloat16),
        grid_spec=pltpu.PrefetchScalarGridSpec(
            num_scalar_prefetch=1,
            grid=(local_pre, HQ, block_query // tq),
            in_specs=[q_spec] + [kv_spec] * n_blocks,
            out_specs=q_spec,
        ),
        compiler_params=pltpu.CompilerParams(
            dimension_semantics=("arbitrary", "arbitrary", "arbitrary")
        ),
        cost_estimate=pl.CostEstimate(
            flops=flops,
            transcendentals=local_pre * HQ * block_query * block * n_blocks,
            bytes_accessed=2 * pre_query.size * 2 + sum(b.size for b in kv_blocks) * 2,
        ),
    )(first_key, pre_query, *kv_blocks)


def body(
    pre_query,
    pre_fresh,
    pre_cache,
    pre_start,
    pre_resid,
    dec_query,
    dec_fresh,
    decode_window_cache,
    dec_length,
    dec_resid,
    out_weight,
    norm_gain,
    embedding,
):
    seq_count = lax.axis_size("seq")
    seq_index = lax.axis_index("seq")
    local_pre = pre_query.shape[0]
    block_query = pre_query.shape[1]
    score_scale = HEAD_SIZE ** (-0.5)
    kv_blocks = [None] * (seq_count + 1)
    kv_blocks[0] = pre_cache
    kv_blocks[seq_count] = pre_fresh
    for shift in range(1, seq_count):
        outgoing = jnp.where(seq_index + shift <= seq_count - 1, pre_fresh, pre_cache)
        kv_blocks[seq_count - shift] = from_behind(outgoing, "seq", shift)
    first_key = (WIN - seq_index * block_query - pre_start).astype(jnp.int32)
    pre_mixed_3d = prefill_attention(pre_query, kv_blocks, first_key)
    pre_mixed = pre_mixed_3d.reshape(local_pre * block_query, HQ * HEAD_SIZE)
    decode_token_rows = dec_query.reshape(-1, HQ, HEAD_SIZE)
    cache_scores = (
        jnp.einsum(
            "vfx,vzx->vfz",
            decode_token_rows,
            decode_window_cache[:, :, :HEAD_SIZE],
            preferred_element_type=jnp.float32,
        )
        * score_scale
    )
    self_scores = (
        jnp.einsum(
            "bhd,bd->bh",
            decode_token_rows,
            dec_fresh[:, :HEAD_SIZE],
            preferred_element_type=jnp.float32,
        )[:, :, None]
        * score_scale
    )
    slot_index = jnp.arange(WIN, dtype=jnp.int32)[None, :]
    length_col = dec_length[:, None]
    held_pos = length_col - 1 - jnp.mod(length_col - 1 - slot_index, WIN)
    live_mask = ((held_pos >= 0) & (held_pos > length_col - WIN))[:, None, :]
    peak_score = jnp.maximum(
        jnp.max(jnp.where(live_mask, cache_scores, NEG_BIG), axis=2, keepdims=True), self_scores
    )
    cache_attention_weights = jnp.where(live_mask, jnp.exp(cache_scores - peak_score), 0.0)
    self_weights = jnp.exp(self_scores - peak_score)
    denom_sum = jnp.sum(cache_attention_weights, axis=2, keepdims=True) + self_weights
    self_rounded = lax.optimization_barrier(self_weights.astype(jnp.bfloat16)).astype(jnp.float32)
    cache_part = jnp.einsum(
        "ect,ety->ecy",
        cache_attention_weights.astype(jnp.bfloat16),
        decode_window_cache[:, :, HEAD_SIZE:],
        preferred_element_type=jnp.float32,
    )
    self_part = self_rounded * dec_fresh[:, None, HEAD_SIZE:].astype(jnp.float32)
    dec_mixed = (
        ((cache_part + self_part) / denom_sum).astype(jnp.bfloat16).reshape(-1, HQ * HEAD_SIZE)
    )
    mixed_rows = jnp.concatenate([pre_mixed, dec_mixed], axis=0)
    projected = jnp.dot(
        mixed_rows,
        lax.all_gather(out_weight, "vocab", axis=0, tiled=True),
        preferred_element_type=jnp.float32,
    )
    pre_rows = local_pre * block_query
    pre_out = (
        pre_resid.astype(jnp.float32) + projected[:pre_rows].reshape(local_pre, block_query, D)
    ).astype(jnp.bfloat16)
    dec_out = (dec_resid.astype(jnp.float32) + projected[pre_rows:]).astype(jnp.bfloat16)
    local_dec = dec_mixed.shape[0]
    vocab_count = lax.axis_size("vocab")
    vocab_index = lax.axis_index("vocab")
    weight_rows = out_weight.shape[0]
    head_count = local_dec + local_pre
    head_mixed = jnp.concatenate([dec_mixed, pre_mixed_3d[:, block_query - 1, :]], axis=0)
    head_resid = jnp.concatenate([dec_resid, pre_resid[:, block_query - 1, :]], axis=0)
    group_rows = lax.all_gather(head_mixed, "vocab", axis=0, tiled=True)
    own_columns = lax.dynamic_slice_in_dim(
        group_rows, vocab_index * weight_rows, weight_rows, axis=1
    )
    partial = jnp.dot(own_columns, out_weight, preferred_element_type=jnp.float32)
    pieces = lax.all_to_all(
        partial.reshape(vocab_count, head_count, D), "vocab", 0, 0, tiled=True
    )
    head_proj = jnp.sum(pieces, axis=0)
    head_in = (head_resid.astype(jnp.float32) + head_proj).astype(jnp.bfloat16)
    everyone = gather_all(normalize(head_in, norm_gain))
    layout = everyone.reshape(seq_count, vocab_count, head_count, D)
    decode_all = layout[:, :, :local_dec].reshape(-1, D)
    prefill_every_request = layout[seq_count - 1, :, local_dec:].reshape(-1, D)
    head_rows = jnp.concatenate([decode_all, prefill_every_request], axis=0)
    logits = lax.dot_general(
        head_rows, embedding, (((1,), (1,)), ((), ())), preferred_element_type=jnp.float32
    )
    local_peak = jnp.max(logits, axis=1)
    local_sum = jnp.sum(jnp.exp(logits - local_peak[:, None]), axis=1)
    stats = gather_all(jnp.stack([local_peak, local_sum])[None])
    global_peak = jnp.max(stats[:, 0], axis=0)
    global_sum = jnp.sum(stats[:, 1] * jnp.exp(stats[:, 0] - global_peak[None]), axis=0)
    total = (global_peak + jnp.log(global_sum))[:, None]
    log_probs = (logits - total).astype(jnp.bfloat16)
    dec_count = decode_all.shape[0]
    return (pre_out, dec_out, log_probs[:dec_count], log_probs[dec_count:])


def solution(mesh):
    in_specs = (
        P("vocab", "seq", None),
        P("vocab", "seq", None),
        P("vocab", "seq", None),
        P("vocab"),
        P("vocab", "seq", None),
        P(("seq", "vocab"), None),
        P(("seq", "vocab"), None),
        P(("seq", "vocab"), None, None),
        P(("seq", "vocab")),
        P(("seq", "vocab"), None),
        P("vocab", None),
        P(),
        P(("seq", "vocab"), None),
    )
    out_specs = (
        P("vocab", "seq", None),
        P(("seq", "vocab"), None),
        P(None, ("seq", "vocab")),
        P(None, ("seq", "vocab")),
    )
    return jax.shard_map(body, mesh=mesh, in_specs=in_specs, out_specs=out_specs, check_vma=False)
```

```python
import functools

import jax
import jax.numpy as jnp
from jax import lax
from jax.experimental import pallas as pl
from jax.experimental.pallas import tpu as pltpu
from jax.sharding import PartitionSpec as P

D = 2560
HQ = 10
HEAD_SIZE = 256
WIN = 2048


NEG_BIG = -1e30
STABILITY_FLOOR = 1e-06


def from_behind(value, axis, steps):
    count = lax.axis_size(axis)
    pairs = [(source, (source + steps) % count) for source in range(count)]
    return lax.ppermute(value, axis, pairs)


def gather_all(value):
    inner = lax.all_gather(value, "vocab", axis=0, tiled=True)
    return lax.all_gather(inner, "seq", axis=0, tiled=True)


def doubling_gather(value, axis, tie=None):
    count = lax.axis_size(axis)
    if count & (count - 1):
        return lax.all_gather(value, axis, axis=0, tiled=True), tie
    index = lax.axis_index(axis)
    tie_out = None
    step = 1
    while step < count:
        pairs = [(source, source ^ step) for source in range(count)]
        theirs = lax.ppermute(value, axis, pairs)
        if tie is not None:
            theirs, tie = lax.optimization_barrier((theirs, tie))
            tie_out, tie = tie, None
        upper = (index // step) % 2 == 1
        value = jnp.where(
            upper,
            jnp.concatenate([theirs, value], axis=0),
            jnp.concatenate([value, theirs], axis=0),
        )
        step *= 2
    if tie is not None:
        return value, tie
    return value, tie_out


def normalize(rows_in, gain):
    values = rows_in.astype(jnp.float32)
    square_mean = jnp.mean(values * values, axis=-1, keepdims=True)
    return (values * lax.rsqrt(square_mean + STABILITY_FLOOR) * gain).astype(jnp.bfloat16)


def prefill_kernel(t0_ref, q_ref, *refs, n_blocks, block, tq):
    kv_refs = refs[:n_blocks]
    o_ref = refs[n_blocks]
    r = pl.program_id(0)
    qi = pl.program_id(2)
    t0 = t0_ref[r]
    q = q_ref[0]
    row = qi * tq + lax.broadcasted_iota(jnp.int32, (tq, block), 0)
    col = lax.broadcasted_iota(jnp.int32, (tq, block), 1)
    peak = jnp.full((tq, 1), NEG_BIG, jnp.float32)
    denom = jnp.zeros((tq, 1), jnp.float32)
    accum = jnp.zeros((tq, HEAD_SIZE), jnp.float32)
    scale = HEAD_SIZE ** (-0.5)
    for j in range(n_blocks):
        kv = kv_refs[j]
        keys = kv[0, :, :HEAD_SIZE]
        values = kv[0, :, HEAD_SIZE:]
        scores = (
            lax.dot_general(
                q, keys, (((1,), (1,)), ((), ())), preferred_element_type=jnp.float32
            )
            * scale
        )
        t = j * block + col
        if j == 0 or j == n_blocks - 1:
            valid = t >= t0
            if j == 0:
                valid = valid & (t > row)
            else:
                valid = valid & (t <= row + WIN)
            scores = jnp.where(valid, scores, NEG_BIG)
        else:
            key = j * block + lax.broadcasted_iota(jnp.int32, (1, block), 1)
            scores = scores + jnp.where(key >= t0, 0.0, NEG_BIG)
        peak_new = jnp.maximum(peak, jnp.max(scores, axis=1, keepdims=True))
        weights = jnp.exp(scores - peak_new)
        decay = jnp.exp(peak - peak_new)
        denom = denom * decay + jnp.sum(weights, axis=1, keepdims=True)
        accum = accum * decay + jnp.dot(
            weights.astype(jnp.bfloat16), values, preferred_element_type=jnp.float32
        )
        peak = peak_new
    o_ref[0] = (accum / denom).astype(o_ref.dtype)


def prefill_attention(pre_query, kv_blocks, first_key):
    local_pre, block_query, _ = pre_query.shape
    block = kv_blocks[0].shape[1]
    n_blocks = len(kv_blocks)
    tq = min(block_query, 512)
    kernel = functools.partial(prefill_kernel, n_blocks=n_blocks, block=block, tq=tq)
    kv_spec = pl.BlockSpec((1, block, 2 * HEAD_SIZE), lambda r, h, qi, t0: (r, 0, 0))
    q_spec = pl.BlockSpec((1, tq, HEAD_SIZE), lambda r, h, qi, t0: (r, qi, h))
    flops = 4 * local_pre * HQ * block_query * block * n_blocks * HEAD_SIZE
    return pl.pallas_call(
        kernel,
        out_shape=jax.ShapeDtypeStruct(pre_query.shape, jnp.bfloat16),
        grid_spec=pltpu.PrefetchScalarGridSpec(
            num_scalar_prefetch=1,
            grid=(local_pre, HQ, block_query // tq),
            in_specs=[q_spec] + [kv_spec] * n_blocks,
            out_specs=q_spec,
        ),
        compiler_params=pltpu.CompilerParams(
            dimension_semantics=("arbitrary", "arbitrary", "arbitrary")
        ),
        cost_estimate=pl.CostEstimate(
            flops=flops,
            transcendentals=local_pre * HQ * block_query * block * n_blocks,
            bytes_accessed=2 * pre_query.size * 2 + sum(b.size for b in kv_blocks) * 2,
        ),
    )(first_key, pre_query, *kv_blocks)


def body(
    pre_query,
    pre_fresh,
    pre_cache,
    pre_start,
    pre_resid,
    dec_query,
    dec_fresh,
    decode_window_cache,
    dec_length,
    dec_resid,
    out_weight,
    norm_gain,
    embedding,
):
    seq_count = lax.axis_size("seq")
    seq_index = lax.axis_index("seq")
    local_pre = pre_query.shape[0]
    block_query = pre_query.shape[1]
    score_scale = HEAD_SIZE ** (-0.5)
    kv_blocks = [None] * (seq_count + 1)
    kv_blocks[0] = pre_cache
    kv_blocks[seq_count] = pre_fresh
    for shift in range(1, seq_count):
        outgoing = jnp.where(seq_index + shift <= seq_count - 1, pre_fresh, pre_cache)
        kv_blocks[seq_count - shift] = from_behind(outgoing, "seq", shift)
    first_key = (WIN - seq_index * block_query - pre_start).astype(jnp.int32)
    pre_mixed_3d = prefill_attention(pre_query, kv_blocks, first_key)
    pre_mixed = pre_mixed_3d.reshape(local_pre * block_query, HQ * HEAD_SIZE)
    decode_token_rows = dec_query.reshape(-1, HQ, HEAD_SIZE)
    cache_scores = (
        jnp.einsum(
            "vfx,vzx->vfz",
            decode_token_rows,
            decode_window_cache[:, :, :HEAD_SIZE],
            preferred_element_type=jnp.float32,
        )
        * score_scale
    )
    self_scores = (
        jnp.einsum(
            "bhd,bd->bh",
            decode_token_rows,
            dec_fresh[:, :HEAD_SIZE],
            preferred_element_type=jnp.float32,
        )[:, :, None]
        * score_scale
    )
    slot_index = jnp.arange(WIN, dtype=jnp.int32)[None, :]
    length_col = dec_length[:, None]
    held_pos = length_col - 1 - jnp.mod(length_col - 1 - slot_index, WIN)
    live_mask = ((held_pos >= 0) & (held_pos > length_col - WIN))[:, None, :]
    peak_score = jnp.maximum(
        jnp.max(jnp.where(live_mask, cache_scores, NEG_BIG), axis=2, keepdims=True), self_scores
    )
    cache_attention_weights = jnp.where(live_mask, jnp.exp(cache_scores - peak_score), 0.0)
    self_weights = jnp.exp(self_scores - peak_score)
    denom_sum = jnp.sum(cache_attention_weights, axis=2, keepdims=True) + self_weights
    self_rounded = lax.optimization_barrier(self_weights.astype(jnp.bfloat16)).astype(jnp.float32)
    cache_part = jnp.einsum(
        "ect,ety->ecy",
        cache_attention_weights.astype(jnp.bfloat16),
        decode_window_cache[:, :, HEAD_SIZE:],
        preferred_element_type=jnp.float32,
    )
    self_part = self_rounded * dec_fresh[:, None, HEAD_SIZE:].astype(jnp.float32)
    dec_mixed = (
        ((cache_part + self_part) / denom_sum).astype(jnp.bfloat16).reshape(-1, HQ * HEAD_SIZE)
    )
    mixed_rows = jnp.concatenate([pre_mixed, dec_mixed], axis=0)
    projected = jnp.dot(
        mixed_rows,
        lax.all_gather(out_weight, "vocab", axis=0, tiled=True),
        preferred_element_type=jnp.float32,
    )
    pre_rows = local_pre * block_query
    pre_out = (
        pre_resid.astype(jnp.float32) + projected[:pre_rows].reshape(local_pre, block_query, D)
    ).astype(jnp.bfloat16)
    dec_out = (dec_resid.astype(jnp.float32) + projected[pre_rows:]).astype(jnp.bfloat16)
    local_dec = dec_mixed.shape[0]
    vocab_count = lax.axis_size("vocab")
    vocab_index = lax.axis_index("vocab")
    weight_rows = out_weight.shape[0]
    head_count = local_dec + local_pre
    head_mixed = jnp.concatenate([dec_mixed, pre_mixed_3d[:, block_query - 1, :]], axis=0)
    head_resid = jnp.concatenate([dec_resid, pre_resid[:, block_query - 1, :]], axis=0)
    group_rows = lax.all_gather(head_mixed, "vocab", axis=0, tiled=True)
    own_columns = lax.dynamic_slice_in_dim(
        group_rows, vocab_index * weight_rows, weight_rows, axis=1
    )
    partial = jnp.dot(own_columns, out_weight, preferred_element_type=jnp.float32)
    pieces = lax.all_to_all(
        partial.reshape(vocab_count, head_count, D), "vocab", 0, 0, tiled=True
    )
    head_proj = jnp.sum(pieces, axis=0)
    head_in = (head_resid.astype(jnp.float32) + head_proj).astype(jnp.bfloat16)
    everyone = gather_all(normalize(head_in, norm_gain))
    layout = everyone.reshape(seq_count, vocab_count, head_count, D)
    decode_all = layout[:, :, :local_dec].reshape(-1, D)
    prefill_every_request = layout[seq_count - 1, :, local_dec:].reshape(-1, D)
    head_rows = jnp.concatenate([decode_all, prefill_every_request], axis=0)
    logits = lax.dot_general(
        head_rows, embedding, (((1,), (1,)), ((), ())), preferred_element_type=jnp.float32
    )
    local_peak = jnp.max(logits, axis=1)
    local_sum = jnp.sum(jnp.exp(logits - local_peak[:, None]), axis=1)
    own_stats = jnp.stack([local_peak, local_sum])[None]
    vocab_stats, (pre_out, dec_out) = doubling_gather(own_stats, "vocab", (pre_out, dec_out))
    stats, _ = doubling_gather(vocab_stats, "seq")
    global_peak = jnp.max(stats[:, 0], axis=0)
    global_sum = jnp.sum(stats[:, 1] * jnp.exp(stats[:, 0] - global_peak[None]), axis=0)
    total = (global_peak + jnp.log(global_sum))[:, None]
    log_probs = (logits - total).astype(jnp.bfloat16)
    dec_count = decode_all.shape[0]
    return (pre_out, dec_out, log_probs[:dec_count], log_probs[dec_count:])


def solution(mesh):
    in_specs = (
        P("vocab", "seq", None),
        P("vocab", "seq", None),
        P("vocab", "seq", None),
        P("vocab"),
        P("vocab", "seq", None),
        P(("seq", "vocab"), None),
        P(("seq", "vocab"), None),
        P(("seq", "vocab"), None, None),
        P(("seq", "vocab")),
        P(("seq", "vocab"), None),
        P("vocab", None),
        P(),
        P(("seq", "vocab"), None),
    )
    out_specs = (
        P("vocab", "seq", None),
        P(("seq", "vocab"), None),
        P(None, ("seq", "vocab")),
        P(None, ("seq", "vocab")),
    )
    return jax.shard_map(body, mesh=mesh, in_specs=in_specs, out_specs=out_specs, check_vma=False)
```

```python
import functools

import jax
import jax.numpy as jnp
from jax import lax
from jax.experimental import pallas as pl
from jax.experimental.pallas import tpu as pltpu
from jax.sharding import PartitionSpec as P

D = 2560
HQ = 10
HEAD_SIZE = 256
WIN = 2048


NEG_BIG = -1e30
STABILITY_FLOOR = 1e-06


def from_behind(value, axis, steps):
    count = lax.axis_size(axis)
    pairs = [(source, (source + steps) % count) for source in range(count)]
    return lax.ppermute(value, axis, pairs)


def gather_all(value):
    inner, _ = doubling_gather(value, "vocab")
    return doubling_gather(inner, "seq")[0]


def doubling_gather(value, axis, tie=None):
    count = lax.axis_size(axis)
    if count & (count - 1):
        return lax.all_gather(value, axis, axis=0, tiled=True), tie
    index = lax.axis_index(axis)
    tie_out = None
    step = 1
    while step < count:
        pairs = [(source, source ^ step) for source in range(count)]
        theirs = lax.ppermute(value, axis, pairs)
        if tie is not None:
            theirs, tie = lax.optimization_barrier((theirs, tie))
            tie_out, tie = tie, None
        upper = (index // step) % 2 == 1
        value = jnp.where(
            upper,
            jnp.concatenate([theirs, value], axis=0),
            jnp.concatenate([value, theirs], axis=0),
        )
        step *= 2
    if tie is not None:
        return value, tie
    return value, tie_out


def normalize(rows_in, gain):
    values = rows_in.astype(jnp.float32)
    square_mean = jnp.mean(values * values, axis=-1, keepdims=True)
    return (values * lax.rsqrt(square_mean + STABILITY_FLOOR) * gain).astype(jnp.bfloat16)


def prefill_kernel(t0_ref, q_ref, *refs, n_blocks, block, tq):
    kv_refs = refs[:n_blocks]
    o_ref = refs[n_blocks]
    r = pl.program_id(0)
    qi = pl.program_id(2)
    t0 = t0_ref[r]
    q = q_ref[0]
    row = qi * tq + lax.broadcasted_iota(jnp.int32, (tq, block), 0)
    col = lax.broadcasted_iota(jnp.int32, (tq, block), 1)
    peak = jnp.full((tq, 1), NEG_BIG, jnp.float32)
    denom = jnp.zeros((tq, 1), jnp.float32)
    accum = jnp.zeros((tq, HEAD_SIZE), jnp.float32)
    scale = HEAD_SIZE ** (-0.5)
    for j in range(n_blocks):
        kv = kv_refs[j]
        keys = kv[0, :, :HEAD_SIZE]
        values = kv[0, :, HEAD_SIZE:]
        scores = (
            lax.dot_general(
                q, keys, (((1,), (1,)), ((), ())), preferred_element_type=jnp.float32
            )
            * scale
        )
        t = j * block + col
        if j == 0 or j == n_blocks - 1:
            valid = t >= t0
            if j == 0:
                valid = valid & (t > row)
            else:
                valid = valid & (t <= row + WIN)
            scores = jnp.where(valid, scores, NEG_BIG)
        else:
            key = j * block + lax.broadcasted_iota(jnp.int32, (1, block), 1)
            scores = scores + jnp.where(key >= t0, 0.0, NEG_BIG)
        peak_new = jnp.maximum(peak, jnp.max(scores, axis=1, keepdims=True))
        weights = jnp.exp(scores - peak_new)
        decay = jnp.exp(peak - peak_new)
        denom = denom * decay + jnp.sum(weights, axis=1, keepdims=True)
        accum = accum * decay + jnp.dot(
            weights.astype(jnp.bfloat16), values, preferred_element_type=jnp.float32
        )
        peak = peak_new
    o_ref[0] = (accum / denom).astype(o_ref.dtype)


def prefill_attention(pre_query, kv_blocks, first_key):
    local_pre, block_query, _ = pre_query.shape
    block = kv_blocks[0].shape[1]
    n_blocks = len(kv_blocks)
    tq = min(block_query, 512)
    kernel = functools.partial(prefill_kernel, n_blocks=n_blocks, block=block, tq=tq)
    kv_spec = pl.BlockSpec((1, block, 2 * HEAD_SIZE), lambda r, h, qi, t0: (r, 0, 0))
    q_spec = pl.BlockSpec((1, tq, HEAD_SIZE), lambda r, h, qi, t0: (r, qi, h))
    flops = 4 * local_pre * HQ * block_query * block * n_blocks * HEAD_SIZE
    return pl.pallas_call(
        kernel,
        out_shape=jax.ShapeDtypeStruct(pre_query.shape, jnp.bfloat16),
        grid_spec=pltpu.PrefetchScalarGridSpec(
            num_scalar_prefetch=1,
            grid=(local_pre, HQ, block_query // tq),
            in_specs=[q_spec] + [kv_spec] * n_blocks,
            out_specs=q_spec,
        ),
        compiler_params=pltpu.CompilerParams(
            dimension_semantics=("arbitrary", "arbitrary", "arbitrary")
        ),
        cost_estimate=pl.CostEstimate(
            flops=flops,
            transcendentals=local_pre * HQ * block_query * block * n_blocks,
            bytes_accessed=2 * pre_query.size * 2 + sum(b.size for b in kv_blocks) * 2,
        ),
    )(first_key, pre_query, *kv_blocks)


def body(
    pre_query,
    pre_fresh,
    pre_cache,
    pre_start,
    pre_resid,
    dec_query,
    dec_fresh,
    decode_window_cache,
    dec_length,
    dec_resid,
    out_weight,
    norm_gain,
    embedding,
):
    seq_count = lax.axis_size("seq")
    seq_index = lax.axis_index("seq")
    local_pre = pre_query.shape[0]
    block_query = pre_query.shape[1]
    score_scale = HEAD_SIZE ** (-0.5)
    kv_blocks = [None] * (seq_count + 1)
    kv_blocks[0] = pre_cache
    kv_blocks[seq_count] = pre_fresh
    for shift in range(1, seq_count):
        outgoing = jnp.where(seq_index + shift <= seq_count - 1, pre_fresh, pre_cache)
        kv_blocks[seq_count - shift] = from_behind(outgoing, "seq", shift)
    first_key = (WIN - seq_index * block_query - pre_start).astype(jnp.int32)
    pre_mixed_3d = prefill_attention(pre_query, kv_blocks, first_key)
    pre_mixed = pre_mixed_3d.reshape(local_pre * block_query, HQ * HEAD_SIZE)
    decode_token_rows = dec_query.reshape(-1, HQ, HEAD_SIZE)
    cache_scores = (
        jnp.einsum(
            "vfx,vzx->vfz",
            decode_token_rows,
            decode_window_cache[:, :, :HEAD_SIZE],
            preferred_element_type=jnp.float32,
        )
        * score_scale
    )
    self_scores = (
        jnp.einsum(
            "bhd,bd->bh",
            decode_token_rows,
            dec_fresh[:, :HEAD_SIZE],
            preferred_element_type=jnp.float32,
        )[:, :, None]
        * score_scale
    )
    slot_index = jnp.arange(WIN, dtype=jnp.int32)[None, :]
    length_col = dec_length[:, None]
    held_pos = length_col - 1 - jnp.mod(length_col - 1 - slot_index, WIN)
    live_mask = ((held_pos >= 0) & (held_pos > length_col - WIN))[:, None, :]
    peak_score = jnp.maximum(
        jnp.max(jnp.where(live_mask, cache_scores, NEG_BIG), axis=2, keepdims=True), self_scores
    )
    cache_attention_weights = jnp.where(live_mask, jnp.exp(cache_scores - peak_score), 0.0)
    self_weights = jnp.exp(self_scores - peak_score)
    denom_sum = jnp.sum(cache_attention_weights, axis=2, keepdims=True) + self_weights
    self_rounded = lax.optimization_barrier(self_weights.astype(jnp.bfloat16)).astype(jnp.float32)
    cache_part = jnp.einsum(
        "ect,ety->ecy",
        cache_attention_weights.astype(jnp.bfloat16),
        decode_window_cache[:, :, HEAD_SIZE:],
        preferred_element_type=jnp.float32,
    )
    self_part = self_rounded * dec_fresh[:, None, HEAD_SIZE:].astype(jnp.float32)
    dec_mixed = (
        ((cache_part + self_part) / denom_sum).astype(jnp.bfloat16).reshape(-1, HQ * HEAD_SIZE)
    )
    mixed_rows = jnp.concatenate([pre_mixed, dec_mixed], axis=0)
    projected = jnp.dot(
        mixed_rows,
        lax.all_gather(out_weight, "vocab", axis=0, tiled=True),
        preferred_element_type=jnp.float32,
    )
    pre_rows = local_pre * block_query
    pre_out = (
        pre_resid.astype(jnp.float32) + projected[:pre_rows].reshape(local_pre, block_query, D)
    ).astype(jnp.bfloat16)
    dec_out = (dec_resid.astype(jnp.float32) + projected[pre_rows:]).astype(jnp.bfloat16)
    local_dec = dec_mixed.shape[0]
    vocab_count = lax.axis_size("vocab")
    vocab_index = lax.axis_index("vocab")
    weight_rows = out_weight.shape[0]
    head_count = local_dec + local_pre
    head_mixed = jnp.concatenate([dec_mixed, pre_mixed_3d[:, block_query - 1, :]], axis=0)
    head_resid = jnp.concatenate([dec_resid, pre_resid[:, block_query - 1, :]], axis=0)
    group_rows = lax.all_gather(head_mixed, "vocab", axis=0, tiled=True)
    own_columns = lax.dynamic_slice_in_dim(
        group_rows, vocab_index * weight_rows, weight_rows, axis=1
    )
    partial = jnp.dot(own_columns, out_weight, preferred_element_type=jnp.float32)
    pieces = lax.all_to_all(
        partial.reshape(vocab_count, head_count, D), "vocab", 0, 0, tiled=True
    )
    head_proj = jnp.sum(pieces, axis=0)
    head_in = (head_resid.astype(jnp.float32) + head_proj).astype(jnp.bfloat16)
    everyone = gather_all(normalize(head_in, norm_gain))
    layout = everyone.reshape(seq_count, vocab_count, head_count, D)
    decode_all = layout[:, :, :local_dec].reshape(-1, D)
    prefill_every_request = layout[seq_count - 1, :, local_dec:].reshape(-1, D)
    head_rows = jnp.concatenate([decode_all, prefill_every_request], axis=0)
    logits = lax.dot_general(
        head_rows, embedding, (((1,), (1,)), ((), ())), preferred_element_type=jnp.float32
    )
    local_peak = jnp.max(logits, axis=1)
    local_sum = jnp.sum(jnp.exp(logits - local_peak[:, None]), axis=1)
    own_stats = jnp.stack([local_peak, local_sum])[None]
    vocab_stats, (pre_out, dec_out) = doubling_gather(own_stats, "vocab", (pre_out, dec_out))
    stats, _ = doubling_gather(vocab_stats, "seq")
    global_peak = jnp.max(stats[:, 0], axis=0)
    global_sum = jnp.sum(stats[:, 1] * jnp.exp(stats[:, 0] - global_peak[None]), axis=0)
    total = (global_peak + jnp.log(global_sum))[:, None]
    log_probs = (logits - total).astype(jnp.bfloat16)
    dec_count = decode_all.shape[0]
    return (pre_out, dec_out, log_probs[:dec_count], log_probs[dec_count:])


def solution(mesh):
    in_specs = (
        P("vocab", "seq", None),
        P("vocab", "seq", None),
        P("vocab", "seq", None),
        P("vocab"),
        P("vocab", "seq", None),
        P(("seq", "vocab"), None),
        P(("seq", "vocab"), None),
        P(("seq", "vocab"), None, None),
        P(("seq", "vocab")),
        P(("seq", "vocab"), None),
        P("vocab", None),
        P(),
        P(("seq", "vocab"), None),
    )
    out_specs = (
        P("vocab", "seq", None),
        P(("seq", "vocab"), None),
        P(None, ("seq", "vocab")),
        P(None, ("seq", "vocab")),
    )
    return jax.shard_map(body, mesh=mesh, in_specs=in_specs, out_specs=out_specs, check_vma=False)
```

```python
import functools

import jax
import jax.numpy as jnp
from jax import lax
from jax.experimental import pallas as pl
from jax.experimental.pallas import tpu as pltpu
from jax.sharding import PartitionSpec as P

D = 2560
HQ = 10
HEAD_SIZE = 256
WIN = 2048


NEG_BIG = -1e30
STABILITY_FLOOR = 1e-06


def from_behind(value, axis, steps):
    count = lax.axis_size(axis)
    pairs = [(source, (source + steps) % count) for source in range(count)]
    return lax.ppermute(value, axis, pairs)


def gather_all(value):
    inner = lax.all_gather(value, "vocab", axis=0, tiled=True)
    return lax.all_gather(inner, "seq", axis=0, tiled=True)


def doubling_gather(value, axis, tie=None):
    count = lax.axis_size(axis)
    if count & (count - 1):
        return lax.all_gather(value, axis, axis=0, tiled=True), tie
    index = lax.axis_index(axis)
    tie_out = None
    step = 1
    while step < count:
        pairs = [(source, source ^ step) for source in range(count)]
        theirs = lax.ppermute(value, axis, pairs)
        if tie is not None:
            theirs, tie = lax.optimization_barrier((theirs, tie))
            tie_out, tie = tie, None
        upper = (index // step) % 2 == 1
        value = jnp.where(
            upper,
            jnp.concatenate([theirs, value], axis=0),
            jnp.concatenate([value, theirs], axis=0),
        )
        step *= 2
    if tie is not None:
        return value, tie
    return value, tie_out


def normalize(rows_in, gain):
    values = rows_in.astype(jnp.float32)
    square_mean = jnp.mean(values * values, axis=-1, keepdims=True)
    return (values * lax.rsqrt(square_mean + STABILITY_FLOOR) * gain).astype(jnp.bfloat16)


def prefill_kernel(t0_ref, q_ref, *refs, positions, n_blocks, block, tq, carry_in, final):
    n_in = len(positions)
    if carry_in:
        peak_ref, denom_ref, accum_ref = refs[:3]
        refs = refs[3:]
    kv_refs = refs[:n_in]
    out_refs = refs[n_in:]
    r = pl.program_id(0)
    qi = pl.program_id(2)
    t0 = t0_ref[r]
    q = q_ref[0]
    row = qi * tq + lax.broadcasted_iota(jnp.int32, (tq, block), 0)
    col = lax.broadcasted_iota(jnp.int32, (tq, block), 1)
    if carry_in:
        peak = peak_ref[0, 0][:, :1]
        denom = denom_ref[0, 0][:, :1]
        accum = accum_ref[0, 0]
    else:
        peak = jnp.full((tq, 1), NEG_BIG, jnp.float32)
        denom = jnp.zeros((tq, 1), jnp.float32)
        accum = jnp.zeros((tq, HEAD_SIZE), jnp.float32)
    scale = HEAD_SIZE ** (-0.5)
    for kv, j in zip(kv_refs, positions):
        keys = kv[0, :, :HEAD_SIZE]
        values = kv[0, :, HEAD_SIZE:]
        scores = (
            lax.dot_general(
                q, keys, (((1,), (1,)), ((), ())), preferred_element_type=jnp.float32
            )
            * scale
        )
        t = j * block + col
        if j == 0 or j == n_blocks - 1:
            valid = t >= t0
            if j == 0:
                valid = valid & (t > row)
            else:
                valid = valid & (t <= row + WIN)
            scores = jnp.where(valid, scores, NEG_BIG)
        else:
            key = j * block + lax.broadcasted_iota(jnp.int32, (1, block), 1)
            scores = scores + jnp.where(key >= t0, 0.0, NEG_BIG)
        peak_new = jnp.maximum(peak, jnp.max(scores, axis=1, keepdims=True))
        weights = jnp.exp(scores - peak_new)
        decay = jnp.exp(peak - peak_new)
        denom = denom * decay + jnp.sum(weights, axis=1, keepdims=True)
        accum = accum * decay + jnp.dot(
            weights.astype(jnp.bfloat16), values, preferred_element_type=jnp.float32
        )
        peak = peak_new
    if final:
        out_refs[0][0] = (accum / denom).astype(out_refs[0].dtype)
    else:
        out_refs[0][0, 0] = jnp.broadcast_to(peak, (tq, 128))
        out_refs[1][0, 0] = jnp.broadcast_to(denom, (tq, 128))
        out_refs[2][0, 0] = accum


def prefill_pass(pre_query, kv_blocks, positions, n_blocks, first_key, carry, final):
    local_pre, block_query, _ = pre_query.shape
    block = kv_blocks[0].shape[1]
    tq = min(block_query, 512)
    kernel = functools.partial(
        prefill_kernel,
        positions=tuple(positions),
        n_blocks=n_blocks,
        block=block,
        tq=tq,
        carry_in=carry is not None,
        final=final,
    )
    kv_spec = pl.BlockSpec((1, block, 2 * HEAD_SIZE), lambda r, h, qi, t0: (r, 0, 0))
    q_spec = pl.BlockSpec((1, tq, HEAD_SIZE), lambda r, h, qi, t0: (r, qi, h))
    stat_spec = pl.BlockSpec((1, 1, tq, 128), lambda r, h, qi, t0: (r, h, qi, 0))
    accum_spec = pl.BlockSpec((1, 1, tq, HEAD_SIZE), lambda r, h, qi, t0: (r, h, qi, 0))
    stat_shape = jax.ShapeDtypeStruct((local_pre, HQ, block_query, 128), jnp.float32)
    accum_shape = jax.ShapeDtypeStruct((local_pre, HQ, block_query, HEAD_SIZE), jnp.float32)
    carry_specs = [] if carry is None else [stat_spec, stat_spec, accum_spec]
    carry_args = [] if carry is None else list(carry)
    if final:
        out_shape = jax.ShapeDtypeStruct(pre_query.shape, jnp.bfloat16)
        out_specs = q_spec
    else:
        out_shape = (stat_shape, stat_shape, accum_shape)
        out_specs = (stat_spec, stat_spec, accum_spec)
    n_in = len(kv_blocks)
    flops = 4 * local_pre * HQ * block_query * block * n_in * HEAD_SIZE
    return pl.pallas_call(
        kernel,
        out_shape=out_shape,
        grid_spec=pltpu.PrefetchScalarGridSpec(
            num_scalar_prefetch=1,
            grid=(local_pre, HQ, block_query // tq),
            in_specs=[q_spec] + carry_specs + [kv_spec] * n_in,
            out_specs=out_specs,
        ),
        compiler_params=pltpu.CompilerParams(
            dimension_semantics=("arbitrary", "arbitrary", "arbitrary")
        ),
        cost_estimate=pl.CostEstimate(
            flops=flops,
            transcendentals=local_pre * HQ * block_query * block * n_in,
            bytes_accessed=2 * pre_query.size * 2 + sum(b.size for b in kv_blocks) * 2,
        ),
    )(first_key, pre_query, *carry_args, *kv_blocks)


def prefill_attention(pre_query, kv_blocks, first_key):
    n_blocks = len(kv_blocks)
    carry = prefill_pass(
        pre_query, [kv_blocks[0], kv_blocks[-1]], [0, n_blocks - 1], n_blocks,
        first_key, None, False,
    )
    middle = list(range(1, n_blocks - 1))
    return prefill_pass(
        pre_query, [kv_blocks[j] for j in middle], middle, n_blocks, first_key, carry, True
    )


def body(
    pre_query,
    pre_fresh,
    pre_cache,
    pre_start,
    pre_resid,
    dec_query,
    dec_fresh,
    decode_window_cache,
    dec_length,
    dec_resid,
    out_weight,
    norm_gain,
    embedding,
):
    seq_count = lax.axis_size("seq")
    seq_index = lax.axis_index("seq")
    local_pre = pre_query.shape[0]
    block_query = pre_query.shape[1]
    score_scale = HEAD_SIZE ** (-0.5)
    kv_blocks = [None] * (seq_count + 1)
    kv_blocks[0] = pre_cache
    kv_blocks[seq_count] = pre_fresh
    for shift in range(1, seq_count):
        outgoing = jnp.where(seq_index + shift <= seq_count - 1, pre_fresh, pre_cache)
        kv_blocks[seq_count - shift] = from_behind(outgoing, "seq", shift)
    first_key = (WIN - seq_index * block_query - pre_start).astype(jnp.int32)
    pre_mixed_3d = prefill_attention(pre_query, kv_blocks, first_key)
    pre_mixed = pre_mixed_3d.reshape(local_pre * block_query, HQ * HEAD_SIZE)
    decode_token_rows = dec_query.reshape(-1, HQ, HEAD_SIZE)
    cache_scores = (
        jnp.einsum(
            "vfx,vzx->vfz",
            decode_token_rows,
            decode_window_cache[:, :, :HEAD_SIZE],
            preferred_element_type=jnp.float32,
        )
        * score_scale
    )
    self_scores = (
        jnp.einsum(
            "bhd,bd->bh",
            decode_token_rows,
            dec_fresh[:, :HEAD_SIZE],
            preferred_element_type=jnp.float32,
        )[:, :, None]
        * score_scale
    )
    slot_index = jnp.arange(WIN, dtype=jnp.int32)[None, :]
    length_col = dec_length[:, None]
    held_pos = length_col - 1 - jnp.mod(length_col - 1 - slot_index, WIN)
    live_mask = ((held_pos >= 0) & (held_pos > length_col - WIN))[:, None, :]
    peak_score = jnp.maximum(
        jnp.max(jnp.where(live_mask, cache_scores, NEG_BIG), axis=2, keepdims=True), self_scores
    )
    cache_attention_weights = jnp.where(live_mask, jnp.exp(cache_scores - peak_score), 0.0)
    self_weights = jnp.exp(self_scores - peak_score)
    denom_sum = jnp.sum(cache_attention_weights, axis=2, keepdims=True) + self_weights
    self_rounded = lax.optimization_barrier(self_weights.astype(jnp.bfloat16)).astype(jnp.float32)
    cache_part = jnp.einsum(
        "ect,ety->ecy",
        cache_attention_weights.astype(jnp.bfloat16),
        decode_window_cache[:, :, HEAD_SIZE:],
        preferred_element_type=jnp.float32,
    )
    self_part = self_rounded * dec_fresh[:, None, HEAD_SIZE:].astype(jnp.float32)
    dec_mixed = (
        ((cache_part + self_part) / denom_sum).astype(jnp.bfloat16).reshape(-1, HQ * HEAD_SIZE)
    )
    mixed_rows = jnp.concatenate([pre_mixed, dec_mixed], axis=0)
    projected = jnp.dot(
        mixed_rows,
        lax.all_gather(out_weight, "vocab", axis=0, tiled=True),
        preferred_element_type=jnp.float32,
    )
    pre_rows = local_pre * block_query
    pre_out = (
        pre_resid.astype(jnp.float32) + projected[:pre_rows].reshape(local_pre, block_query, D)
    ).astype(jnp.bfloat16)
    dec_out = (dec_resid.astype(jnp.float32) + projected[pre_rows:]).astype(jnp.bfloat16)
    local_dec = dec_mixed.shape[0]
    vocab_count = lax.axis_size("vocab")
    vocab_index = lax.axis_index("vocab")
    weight_rows = out_weight.shape[0]
    head_count = local_dec + local_pre
    head_mixed = jnp.concatenate([dec_mixed, pre_mixed_3d[:, block_query - 1, :]], axis=0)
    head_resid = jnp.concatenate([dec_resid, pre_resid[:, block_query - 1, :]], axis=0)
    group_rows = lax.all_gather(head_mixed, "vocab", axis=0, tiled=True)
    own_columns = lax.dynamic_slice_in_dim(
        group_rows, vocab_index * weight_rows, weight_rows, axis=1
    )
    partial = jnp.dot(own_columns, out_weight, preferred_element_type=jnp.float32)
    pieces = lax.all_to_all(
        partial.reshape(vocab_count, head_count, D), "vocab", 0, 0, tiled=True
    )
    head_proj = jnp.sum(pieces, axis=0)
    head_in = (head_resid.astype(jnp.float32) + head_proj).astype(jnp.bfloat16)
    everyone = gather_all(normalize(head_in, norm_gain))
    layout = everyone.reshape(seq_count, vocab_count, head_count, D)
    decode_all = layout[:, :, :local_dec].reshape(-1, D)
    prefill_every_request = layout[seq_count - 1, :, local_dec:].reshape(-1, D)
    head_rows = jnp.concatenate([decode_all, prefill_every_request], axis=0)
    logits = lax.dot_general(
        head_rows, embedding, (((1,), (1,)), ((), ())), preferred_element_type=jnp.float32
    )
    local_peak = jnp.max(logits, axis=1)
    local_sum = jnp.sum(jnp.exp(logits - local_peak[:, None]), axis=1)
    own_stats = jnp.stack([local_peak, local_sum])[None]
    vocab_stats, (pre_out, dec_out) = doubling_gather(own_stats, "vocab", (pre_out, dec_out))
    stats, _ = doubling_gather(vocab_stats, "seq")
    global_peak = jnp.max(stats[:, 0], axis=0)
    global_sum = jnp.sum(stats[:, 1] * jnp.exp(stats[:, 0] - global_peak[None]), axis=0)
    total = (global_peak + jnp.log(global_sum))[:, None]
    log_probs = (logits - total).astype(jnp.bfloat16)
    dec_count = decode_all.shape[0]
    return (pre_out, dec_out, log_probs[:dec_count], log_probs[dec_count:])


def solution(mesh):
    in_specs = (
        P("vocab", "seq", None),
        P("vocab", "seq", None),
        P("vocab", "seq", None),
        P("vocab"),
        P("vocab", "seq", None),
        P(("seq", "vocab"), None),
        P(("seq", "vocab"), None),
        P(("seq", "vocab"), None, None),
        P(("seq", "vocab")),
        P(("seq", "vocab"), None),
        P("vocab", None),
        P(),
        P(("seq", "vocab"), None),
    )
    out_specs = (
        P("vocab", "seq", None),
        P(("seq", "vocab"), None),
        P(None, ("seq", "vocab")),
        P(None, ("seq", "vocab")),
    )
    return jax.shard_map(body, mesh=mesh, in_specs=in_specs, out_specs=out_specs, check_vma=False)
```

```python
import functools

import jax
import jax.numpy as jnp
from jax import lax
from jax.experimental import pallas as pl
from jax.experimental.pallas import tpu as pltpu
from jax.sharding import PartitionSpec as P

D = 2560
HQ = 10
HEAD_SIZE = 256
WIN = 2048


NEG_BIG = -1e30
STABILITY_FLOOR = 1e-06


def from_behind(value, axis, steps):
    count = lax.axis_size(axis)
    pairs = [(source, (source + steps) % count) for source in range(count)]
    return lax.ppermute(value, axis, pairs)


def gather_all(value):
    inner = lax.all_gather(value, "vocab", axis=0, tiled=True)
    return lax.all_gather(inner, "seq", axis=0, tiled=True)


def doubling_gather(value, axis, tie=None):
    count = lax.axis_size(axis)
    if count & (count - 1):
        return lax.all_gather(value, axis, axis=0, tiled=True), tie
    index = lax.axis_index(axis)
    tie_out = None
    step = 1
    while step < count:
        pairs = [(source, source ^ step) for source in range(count)]
        theirs = lax.ppermute(value, axis, pairs)
        if tie is not None:
            theirs, tie = lax.optimization_barrier((theirs, tie))
            tie_out, tie = tie, None
        upper = (index // step) % 2 == 1
        value = jnp.where(
            upper,
            jnp.concatenate([theirs, value], axis=0),
            jnp.concatenate([value, theirs], axis=0),
        )
        step *= 2
    if tie is not None:
        return value, tie
    return value, tie_out


def normalize(rows_in, gain):
    values = rows_in.astype(jnp.float32)
    square_mean = jnp.mean(values * values, axis=-1, keepdims=True)
    return (values * lax.rsqrt(square_mean + STABILITY_FLOOR) * gain).astype(jnp.bfloat16)


def prefill_kernel(t0_ref, q_ref, *refs, n_blocks, block, tq):
    kv_refs = refs[:n_blocks]
    o_ref = refs[n_blocks]
    r = pl.program_id(0)
    qi = pl.program_id(2)
    t0 = t0_ref[r]
    q = q_ref[0]
    row = qi * tq + lax.broadcasted_iota(jnp.int32, (tq, block), 0)
    col = lax.broadcasted_iota(jnp.int32, (tq, block), 1)
    peak = jnp.full((tq, 1), NEG_BIG, jnp.float32)
    denom = jnp.zeros((tq, 1), jnp.float32)
    accum = jnp.zeros((tq, HEAD_SIZE), jnp.float32)
    scale = HEAD_SIZE ** (-0.5)
    for j in range(n_blocks):
        kv = kv_refs[j]
        keys = kv[0, :, :HEAD_SIZE]
        values = kv[0, :, HEAD_SIZE:]
        scores = (
            lax.dot_general(
                q, keys, (((1,), (1,)), ((), ())), preferred_element_type=jnp.float32
            )
            * scale
        )
        t = j * block + col
        if j == 0 or j == n_blocks - 1:
            valid = t >= t0
            if j == 0:
                valid = valid & (t > row)
            else:
                valid = valid & (t <= row + WIN)
            scores = jnp.where(valid, scores, NEG_BIG)
        else:
            key = j * block + lax.broadcasted_iota(jnp.int32, (1, block), 1)
            scores = scores + jnp.where(key >= t0, 0.0, NEG_BIG)
        peak_new = jnp.maximum(peak, jnp.max(scores, axis=1, keepdims=True))
        weights = jnp.exp(scores - peak_new)
        decay = jnp.exp(peak - peak_new)
        denom = denom * decay + jnp.sum(weights, axis=1, keepdims=True)
        accum = accum * decay + jnp.dot(
            weights.astype(jnp.bfloat16), values, preferred_element_type=jnp.float32
        )
        peak = peak_new
    o_ref[0] = (accum / denom).astype(o_ref.dtype)


def prefill_attention(pre_query, kv_blocks, first_key):
    local_pre, block_query, _ = pre_query.shape
    block = kv_blocks[0].shape[1]
    n_blocks = len(kv_blocks)
    tq = min(block_query, 512)
    kernel = functools.partial(prefill_kernel, n_blocks=n_blocks, block=block, tq=tq)
    kv_spec = pl.BlockSpec((1, block, 2 * HEAD_SIZE), lambda r, h, qi, t0: (r, 0, 0))
    q_spec = pl.BlockSpec((1, tq, HEAD_SIZE), lambda r, h, qi, t0: (r, qi, h))
    flops = 4 * local_pre * HQ * block_query * block * n_blocks * HEAD_SIZE
    return pl.pallas_call(
        kernel,
        out_shape=jax.ShapeDtypeStruct(pre_query.shape, jnp.bfloat16),
        grid_spec=pltpu.PrefetchScalarGridSpec(
            num_scalar_prefetch=1,
            grid=(local_pre, HQ, block_query // tq),
            in_specs=[q_spec] + [kv_spec] * n_blocks,
            out_specs=q_spec,
        ),
        compiler_params=pltpu.CompilerParams(
            dimension_semantics=("arbitrary", "arbitrary", "arbitrary")
        ),
        cost_estimate=pl.CostEstimate(
            flops=flops,
            transcendentals=local_pre * HQ * block_query * block * n_blocks,
            bytes_accessed=2 * pre_query.size * 2 + sum(b.size for b in kv_blocks) * 2,
        ),
    )(first_key, pre_query, *kv_blocks)


def body(
    pre_query,
    pre_fresh,
    pre_cache,
    pre_start,
    pre_resid,
    dec_query,
    dec_fresh,
    decode_window_cache,
    dec_length,
    dec_resid,
    out_weight,
    norm_gain,
    embedding,
):
    seq_count = lax.axis_size("seq")
    seq_index = lax.axis_index("seq")
    local_pre = pre_query.shape[0]
    block_query = pre_query.shape[1]
    score_scale = HEAD_SIZE ** (-0.5)
    kv_blocks = [None] * (seq_count + 1)
    kv_blocks[0] = pre_cache
    kv_blocks[seq_count] = pre_fresh
    for shift in range(1, seq_count):
        outgoing = jnp.where(seq_index + shift <= seq_count - 1, pre_fresh, pre_cache)
        kv_blocks[seq_count - shift] = from_behind(outgoing, "seq", shift)
    first_key = (WIN - seq_index * block_query - pre_start).astype(jnp.int32)
    pre_mixed_3d = prefill_attention(pre_query, kv_blocks, first_key)
    pre_mixed = pre_mixed_3d.reshape(local_pre * block_query, HQ * HEAD_SIZE)
    decode_token_rows = dec_query.reshape(-1, HQ, HEAD_SIZE)
    cache_scores = (
        jnp.einsum(
            "vfx,vzx->vfz",
            decode_token_rows,
            decode_window_cache[:, :, :HEAD_SIZE],
            preferred_element_type=jnp.float32,
        )
        * score_scale
    )
    self_scores = (
        jnp.einsum(
            "bhd,bd->bh",
            decode_token_rows,
            dec_fresh[:, :HEAD_SIZE],
            preferred_element_type=jnp.float32,
        )[:, :, None]
        * score_scale
    )
    slot_index = jnp.arange(WIN, dtype=jnp.int32)[None, :]
    length_col = dec_length[:, None]
    held_pos = length_col - 1 - jnp.mod(length_col - 1 - slot_index, WIN)
    live_mask = ((held_pos >= 0) & (held_pos > length_col - WIN))[:, None, :]
    peak_score = jnp.maximum(
        jnp.max(jnp.where(live_mask, cache_scores, NEG_BIG), axis=2, keepdims=True), self_scores
    )
    cache_attention_weights = jnp.where(live_mask, jnp.exp(cache_scores - peak_score), 0.0)
    self_weights = jnp.exp(self_scores - peak_score)
    denom_sum = jnp.sum(cache_attention_weights, axis=2, keepdims=True) + self_weights
    self_rounded = lax.optimization_barrier(self_weights.astype(jnp.bfloat16)).astype(jnp.float32)
    cache_part = jnp.einsum(
        "ect,ety->ecy",
        cache_attention_weights.astype(jnp.bfloat16),
        decode_window_cache[:, :, HEAD_SIZE:],
        preferred_element_type=jnp.float32,
    )
    self_part = self_rounded * dec_fresh[:, None, HEAD_SIZE:].astype(jnp.float32)
    dec_mixed = (
        ((cache_part + self_part) / denom_sum).astype(jnp.bfloat16).reshape(-1, HQ * HEAD_SIZE)
    )
    mixed_rows = jnp.concatenate([pre_mixed, dec_mixed], axis=0)
    projected = jnp.dot(
        mixed_rows,
        lax.all_gather(out_weight, "vocab", axis=0, tiled=True),
        preferred_element_type=jnp.float32,
    )
    pre_rows = local_pre * block_query
    pre_out = (
        pre_resid.astype(jnp.float32) + projected[:pre_rows].reshape(local_pre, block_query, D)
    ).astype(jnp.bfloat16)
    dec_out = (dec_resid.astype(jnp.float32) + projected[pre_rows:]).astype(jnp.bfloat16)
    local_dec = dec_mixed.shape[0]
    vocab_count = lax.axis_size("vocab")
    vocab_index = lax.axis_index("vocab")
    weight_rows = out_weight.shape[0]
    head_count = local_dec + local_pre
    head_mixed = jnp.concatenate([dec_mixed, pre_mixed_3d[:, block_query - 1, :]], axis=0)
    head_resid = jnp.concatenate([dec_resid, pre_resid[:, block_query - 1, :]], axis=0)
    group_rows = lax.all_gather(head_mixed, "vocab", axis=0, tiled=True)
    own_columns = lax.dynamic_slice_in_dim(
        group_rows, vocab_index * weight_rows, weight_rows, axis=1
    )
    partial = jnp.dot(own_columns, out_weight, preferred_element_type=jnp.float32)
    pieces = lax.all_to_all(
        partial.reshape(vocab_count, head_count, D), "vocab", 0, 0, tiled=True
    )
    head_proj = jnp.sum(pieces, axis=0)
    head_in = (head_resid.astype(jnp.float32) + head_proj).astype(jnp.bfloat16)
    everyone = gather_all(normalize(head_in, norm_gain))
    layout = everyone.reshape(seq_count, vocab_count, head_count, D)
    decode_all = layout[:, :, :local_dec].reshape(-1, D)
    prefill_every_request = layout[seq_count - 1, :, local_dec:].reshape(-1, D)
    head_rows = jnp.concatenate([decode_all, prefill_every_request], axis=0)
    logits = lax.dot_general(
        head_rows, embedding, (((1,), (1,)), ((), ())), preferred_element_type=jnp.float32
    )
    local_peak = jnp.max(logits, axis=1)
    local_sum = jnp.sum(jnp.exp(logits - local_peak[:, None]), axis=1)
    own_stats = jnp.stack([local_peak, local_sum])[None]
    vocab_stats, (pre_out, dec_out) = doubling_gather(own_stats, "vocab", (pre_out, dec_out))
    stats, _ = doubling_gather(vocab_stats, "seq")
    global_peak = jnp.max(stats[:, 0], axis=0)
    global_sum = jnp.sum(stats[:, 1] * jnp.exp(stats[:, 0] - global_peak[None]), axis=0)
    total = (global_peak + jnp.log(global_sum))[:, None]
    dec_count = decode_all.shape[0]
    dec_logp = (logits[:dec_count] - total[:dec_count]).astype(jnp.bfloat16)
    pre_logp = (logits[dec_count:] - total[dec_count:]).astype(jnp.bfloat16)
    return (pre_out, dec_out, dec_logp, pre_logp)


def solution(mesh):
    in_specs = (
        P("vocab", "seq", None),
        P("vocab", "seq", None),
        P("vocab", "seq", None),
        P("vocab"),
        P("vocab", "seq", None),
        P(("seq", "vocab"), None),
        P(("seq", "vocab"), None),
        P(("seq", "vocab"), None, None),
        P(("seq", "vocab")),
        P(("seq", "vocab"), None),
        P("vocab", None),
        P(),
        P(("seq", "vocab"), None),
    )
    out_specs = (
        P("vocab", "seq", None),
        P(("seq", "vocab"), None),
        P(None, ("seq", "vocab")),
        P(None, ("seq", "vocab")),
    )
    return jax.shard_map(body, mesh=mesh, in_specs=in_specs, out_specs=out_specs, check_vma=False)
```

```python
import functools

import jax
import jax.numpy as jnp
from jax import lax
from jax.experimental import pallas as pl
from jax.experimental.pallas import tpu as pltpu
from jax.sharding import PartitionSpec as P

D = 2560
HQ = 10
HEAD_SIZE = 256
WIN = 2048


NEG_BIG = -1e30
STABILITY_FLOOR = 1e-06


def from_behind(value, axis, steps):
    count = lax.axis_size(axis)
    pairs = [(source, (source + steps) % count) for source in range(count)]
    return lax.ppermute(value, axis, pairs)


def gather_all(value):
    inner = lax.all_gather(value, "vocab", axis=0, tiled=True)
    return lax.all_gather(inner, "seq", axis=0, tiled=True)


def doubling_gather(value, axis, tie=None):
    count = lax.axis_size(axis)
    if count & (count - 1):
        return lax.all_gather(value, axis, axis=0, tiled=True), tie
    index = lax.axis_index(axis)
    tie_out = None
    step = 1
    while step < count:
        pairs = [(source, source ^ step) for source in range(count)]
        theirs = lax.ppermute(value, axis, pairs)
        if tie is not None:
            theirs, tie = lax.optimization_barrier((theirs, tie))
            tie_out, tie = tie, None
        upper = (index // step) % 2 == 1
        value = jnp.where(
            upper,
            jnp.concatenate([theirs, value], axis=0),
            jnp.concatenate([value, theirs], axis=0),
        )
        step *= 2
    if tie is not None:
        return value, tie
    return value, tie_out


def normalize(rows_in, gain):
    values = rows_in.astype(jnp.float32)
    square_mean = jnp.mean(values * values, axis=-1, keepdims=True)
    return (values * lax.rsqrt(square_mean + STABILITY_FLOOR) * gain).astype(jnp.bfloat16)


def prefill_kernel(t0_ref, q_ref, *refs, n_blocks, block, tq):
    kv_refs = refs[:n_blocks]
    o_ref = refs[n_blocks]
    r = pl.program_id(0)
    qi = pl.program_id(2)
    t0 = t0_ref[r]
    q = q_ref[0]
    row = qi * tq + lax.broadcasted_iota(jnp.int32, (tq, block), 0)
    col = lax.broadcasted_iota(jnp.int32, (tq, block), 1)
    peak = jnp.full((tq, 1), NEG_BIG, jnp.float32)
    denom = jnp.zeros((tq, 1), jnp.float32)
    accum = jnp.zeros((tq, HEAD_SIZE), jnp.float32)
    scale = HEAD_SIZE ** (-0.5)
    for j in range(n_blocks):
        kv = kv_refs[j]
        keys = kv[0, :, :HEAD_SIZE]
        values = kv[0, :, HEAD_SIZE:]
        scores = (
            lax.dot_general(
                q, keys, (((1,), (1,)), ((), ())), preferred_element_type=jnp.float32
            )
            * scale
        )
        t = j * block + col
        if j == 0 or j == n_blocks - 1:
            valid = t >= t0
            if j == 0:
                valid = valid & (t > row)
            else:
                valid = valid & (t <= row + WIN)
            scores = jnp.where(valid, scores, NEG_BIG)
        else:
            key = j * block + lax.broadcasted_iota(jnp.int32, (1, block), 1)
            scores = scores + jnp.where(key >= t0, 0.0, NEG_BIG)
        peak_new = jnp.maximum(peak, jnp.max(scores, axis=1, keepdims=True))
        weights = jnp.exp(scores - peak_new)
        decay = jnp.exp(peak - peak_new)
        denom = denom * decay + jnp.sum(weights, axis=1, keepdims=True)
        accum = accum * decay + jnp.dot(
            weights.astype(jnp.bfloat16), values, preferred_element_type=jnp.float32
        )
        peak = peak_new
    o_ref[0] = (accum / denom).astype(o_ref.dtype)


def prefill_attention(pre_query, kv_blocks, first_key):
    local_pre, block_query, _ = pre_query.shape
    block = kv_blocks[0].shape[1]
    n_blocks = len(kv_blocks)
    tq = min(block_query, 256)
    kernel = functools.partial(prefill_kernel, n_blocks=n_blocks, block=block, tq=tq)
    kv_spec = pl.BlockSpec((1, block, 2 * HEAD_SIZE), lambda r, h, qi, t0: (r, 0, 0))
    q_spec = pl.BlockSpec((1, tq, HEAD_SIZE), lambda r, h, qi, t0: (r, qi, h))
    flops = 4 * local_pre * HQ * block_query * block * n_blocks * HEAD_SIZE
    return pl.pallas_call(
        kernel,
        out_shape=jax.ShapeDtypeStruct(pre_query.shape, jnp.bfloat16),
        grid_spec=pltpu.PrefetchScalarGridSpec(
            num_scalar_prefetch=1,
            grid=(local_pre, HQ, block_query // tq),
            in_specs=[q_spec] + [kv_spec] * n_blocks,
            out_specs=q_spec,
        ),
        compiler_params=pltpu.CompilerParams(
            dimension_semantics=("arbitrary", "arbitrary", "arbitrary")
        ),
        cost_estimate=pl.CostEstimate(
            flops=flops,
            transcendentals=local_pre * HQ * block_query * block * n_blocks,
            bytes_accessed=2 * pre_query.size * 2 + sum(b.size for b in kv_blocks) * 2,
        ),
    )(first_key, pre_query, *kv_blocks)


def body(
    pre_query,
    pre_fresh,
    pre_cache,
    pre_start,
    pre_resid,
    dec_query,
    dec_fresh,
    decode_window_cache,
    dec_length,
    dec_resid,
    out_weight,
    norm_gain,
    embedding,
):
    seq_count = lax.axis_size("seq")
    seq_index = lax.axis_index("seq")
    local_pre = pre_query.shape[0]
    block_query = pre_query.shape[1]
    score_scale = HEAD_SIZE ** (-0.5)
    kv_blocks = [None] * (seq_count + 1)
    kv_blocks[0] = pre_cache
    kv_blocks[seq_count] = pre_fresh
    for shift in range(1, seq_count):
        outgoing = jnp.where(seq_index + shift <= seq_count - 1, pre_fresh, pre_cache)
        kv_blocks[seq_count - shift] = from_behind(outgoing, "seq", shift)
    first_key = (WIN - seq_index * block_query - pre_start).astype(jnp.int32)
    pre_mixed_3d = prefill_attention(pre_query, kv_blocks, first_key)
    pre_mixed = pre_mixed_3d.reshape(local_pre * block_query, HQ * HEAD_SIZE)
    decode_token_rows = dec_query.reshape(-1, HQ, HEAD_SIZE)
    cache_scores = (
        jnp.einsum(
            "vfx,vzx->vfz",
            decode_token_rows,
            decode_window_cache[:, :, :HEAD_SIZE],
            preferred_element_type=jnp.float32,
        )
        * score_scale
    )
    self_scores = (
        jnp.einsum(
            "bhd,bd->bh",
            decode_token_rows,
            dec_fresh[:, :HEAD_SIZE],
            preferred_element_type=jnp.float32,
        )[:, :, None]
        * score_scale
    )
    slot_index = jnp.arange(WIN, dtype=jnp.int32)[None, :]
    length_col = dec_length[:, None]
    held_pos = length_col - 1 - jnp.mod(length_col - 1 - slot_index, WIN)
    live_mask = ((held_pos >= 0) & (held_pos > length_col - WIN))[:, None, :]
    peak_score = jnp.maximum(
        jnp.max(jnp.where(live_mask, cache_scores, NEG_BIG), axis=2, keepdims=True), self_scores
    )
    cache_attention_weights = jnp.where(live_mask, jnp.exp(cache_scores - peak_score), 0.0)
    self_weights = jnp.exp(self_scores - peak_score)
    denom_sum = jnp.sum(cache_attention_weights, axis=2, keepdims=True) + self_weights
    self_rounded = lax.optimization_barrier(self_weights.astype(jnp.bfloat16)).astype(jnp.float32)
    cache_part = jnp.einsum(
        "ect,ety->ecy",
        cache_attention_weights.astype(jnp.bfloat16),
        decode_window_cache[:, :, HEAD_SIZE:],
        preferred_element_type=jnp.float32,
    )
    self_part = self_rounded * dec_fresh[:, None, HEAD_SIZE:].astype(jnp.float32)
    dec_mixed = (
        ((cache_part + self_part) / denom_sum).astype(jnp.bfloat16).reshape(-1, HQ * HEAD_SIZE)
    )
    mixed_rows = jnp.concatenate([pre_mixed, dec_mixed], axis=0)
    projected = jnp.dot(
        mixed_rows,
        lax.all_gather(out_weight, "vocab", axis=0, tiled=True),
        preferred_element_type=jnp.float32,
    )
    pre_rows = local_pre * block_query
    pre_out = (
        pre_resid.astype(jnp.float32) + projected[:pre_rows].reshape(local_pre, block_query, D)
    ).astype(jnp.bfloat16)
    dec_out = (dec_resid.astype(jnp.float32) + projected[pre_rows:]).astype(jnp.bfloat16)
    local_dec = dec_mixed.shape[0]
    vocab_count = lax.axis_size("vocab")
    vocab_index = lax.axis_index("vocab")
    weight_rows = out_weight.shape[0]
    head_count = local_dec + local_pre
    head_mixed = jnp.concatenate([dec_mixed, pre_mixed_3d[:, block_query - 1, :]], axis=0)
    head_resid = jnp.concatenate([dec_resid, pre_resid[:, block_query - 1, :]], axis=0)
    group_rows = lax.all_gather(head_mixed, "vocab", axis=0, tiled=True)
    own_columns = lax.dynamic_slice_in_dim(
        group_rows, vocab_index * weight_rows, weight_rows, axis=1
    )
    partial = jnp.dot(own_columns, out_weight, preferred_element_type=jnp.float32)
    pieces = lax.all_to_all(
        partial.reshape(vocab_count, head_count, D), "vocab", 0, 0, tiled=True
    )
    head_proj = jnp.sum(pieces, axis=0)
    head_in = (head_resid.astype(jnp.float32) + head_proj).astype(jnp.bfloat16)
    everyone = gather_all(normalize(head_in, norm_gain))
    layout = everyone.reshape(seq_count, vocab_count, head_count, D)
    decode_all = layout[:, :, :local_dec].reshape(-1, D)
    prefill_every_request = layout[seq_count - 1, :, local_dec:].reshape(-1, D)
    head_rows = jnp.concatenate([decode_all, prefill_every_request], axis=0)
    logits = lax.dot_general(
        head_rows, embedding, (((1,), (1,)), ((), ())), preferred_element_type=jnp.float32
    )
    local_peak = jnp.max(logits, axis=1)
    local_sum = jnp.sum(jnp.exp(logits - local_peak[:, None]), axis=1)
    own_stats = jnp.stack([local_peak, local_sum])[None]
    vocab_stats, (pre_out, dec_out) = doubling_gather(own_stats, "vocab", (pre_out, dec_out))
    stats, _ = doubling_gather(vocab_stats, "seq")
    global_peak = jnp.max(stats[:, 0], axis=0)
    global_sum = jnp.sum(stats[:, 1] * jnp.exp(stats[:, 0] - global_peak[None]), axis=0)
    total = (global_peak + jnp.log(global_sum))[:, None]
    dec_count = decode_all.shape[0]
    dec_logp = (logits[:dec_count] - total[:dec_count]).astype(jnp.bfloat16)
    pre_logp = (logits[dec_count:] - total[dec_count:]).astype(jnp.bfloat16)
    return (pre_out, dec_out, dec_logp, pre_logp)


def solution(mesh):
    in_specs = (
        P("vocab", "seq", None),
        P("vocab", "seq", None),
        P("vocab", "seq", None),
        P("vocab"),
        P("vocab", "seq", None),
        P(("seq", "vocab"), None),
        P(("seq", "vocab"), None),
        P(("seq", "vocab"), None, None),
        P(("seq", "vocab")),
        P(("seq", "vocab"), None),
        P("vocab", None),
        P(),
        P(("seq", "vocab"), None),
    )
    out_specs = (
        P("vocab", "seq", None),
        P(("seq", "vocab"), None),
        P(None, ("seq", "vocab")),
        P(None, ("seq", "vocab")),
    )
    return jax.shard_map(body, mesh=mesh, in_specs=in_specs, out_specs=out_specs, check_vma=False)
```

```python
import functools

import jax
import jax.numpy as jnp
from jax import lax
from jax.experimental import pallas as pl
from jax.experimental.pallas import tpu as pltpu
from jax.sharding import PartitionSpec as P

D = 2560
HQ = 10
HEAD_SIZE = 256
WIN = 2048


NEG_BIG = -1e30
STABILITY_FLOOR = 1e-06


def from_behind(value, axis, steps):
    count = lax.axis_size(axis)
    pairs = [(source, (source + steps) % count) for source in range(count)]
    return lax.ppermute(value, axis, pairs)


def gather_all(value):
    inner = lax.all_gather(value, "vocab", axis=0, tiled=True)
    return lax.all_gather(inner, "seq", axis=0, tiled=True)


def doubling_gather(value, axis, tie=None):
    count = lax.axis_size(axis)
    if count & (count - 1):
        return lax.all_gather(value, axis, axis=0, tiled=True), tie
    index = lax.axis_index(axis)
    tie_out = None
    step = 1
    while step < count:
        pairs = [(source, source ^ step) for source in range(count)]
        theirs = lax.ppermute(value, axis, pairs)
        if tie is not None:
            theirs, tie = lax.optimization_barrier((theirs, tie))
            tie_out, tie = tie, None
        upper = (index // step) % 2 == 1
        value = jnp.where(
            upper,
            jnp.concatenate([theirs, value], axis=0),
            jnp.concatenate([value, theirs], axis=0),
        )
        step *= 2
    if tie is not None:
        return value, tie
    return value, tie_out


def normalize(rows_in, gain):
    values = rows_in.astype(jnp.float32)
    square_mean = jnp.mean(values * values, axis=-1, keepdims=True)
    return (values * lax.rsqrt(square_mean + STABILITY_FLOOR) * gain).astype(jnp.bfloat16)


def prefill_kernel(t0_ref, q_ref, *refs, n_blocks, block, tq):
    kv_refs = refs[:n_blocks]
    o_ref = refs[n_blocks]
    r = pl.program_id(0)
    qi = pl.program_id(2)
    t0 = t0_ref[r]
    q = q_ref[0]
    row = qi * tq + lax.broadcasted_iota(jnp.int32, (tq, block), 0)
    col = lax.broadcasted_iota(jnp.int32, (tq, block), 1)
    peak = jnp.full((tq, 1), NEG_BIG, jnp.float32)
    denom = jnp.zeros((tq, 1), jnp.float32)
    accum = jnp.zeros((tq, HEAD_SIZE), jnp.float32)
    scale = HEAD_SIZE ** (-0.5)
    for j in range(n_blocks):
        kv = kv_refs[j]
        keys = kv[0, :, :HEAD_SIZE]
        values = kv[0, :, HEAD_SIZE:]
        scores = (
            lax.dot_general(
                q, keys, (((1,), (1,)), ((), ())), preferred_element_type=jnp.float32
            )
            * scale
        )
        t = j * block + col
        if j == 0 or j == n_blocks - 1:
            valid = t >= t0
            if j == 0:
                valid = valid & (t > row)
            else:
                valid = valid & (t <= row + WIN)
            scores = jnp.where(valid, scores, NEG_BIG)
        else:
            key = j * block + lax.broadcasted_iota(jnp.int32, (1, block), 1)
            scores = scores + jnp.where(key >= t0, 0.0, NEG_BIG)
        peak_new = jnp.maximum(peak, jnp.max(scores, axis=1, keepdims=True))
        weights = jnp.exp(scores - peak_new)
        decay = jnp.exp(peak - peak_new)
        denom = denom * decay + jnp.sum(weights, axis=1, keepdims=True)
        accum = accum * decay + jnp.dot(
            weights.astype(jnp.bfloat16), values, preferred_element_type=jnp.float32
        )
        peak = peak_new
    o_ref[0] = (accum / denom).astype(o_ref.dtype)


def prefill_attention(pre_query, kv_blocks, first_key):
    local_pre, block_query, _ = pre_query.shape
    block = kv_blocks[0].shape[1]
    n_blocks = len(kv_blocks)
    tq = min(block_query, 512)
    kernel = functools.partial(prefill_kernel, n_blocks=n_blocks, block=block, tq=tq)
    kv_spec = pl.BlockSpec((1, block, 2 * HEAD_SIZE), lambda r, h, qi, t0: (r, 0, 0))
    q_spec = pl.BlockSpec((1, tq, HEAD_SIZE), lambda r, h, qi, t0: (r, qi, h))
    flops = 4 * local_pre * HQ * block_query * block * n_blocks * HEAD_SIZE
    return pl.pallas_call(
        kernel,
        out_shape=jax.ShapeDtypeStruct(pre_query.shape, jnp.bfloat16),
        grid_spec=pltpu.PrefetchScalarGridSpec(
            num_scalar_prefetch=1,
            grid=(local_pre, HQ, block_query // tq),
            in_specs=[q_spec] + [kv_spec] * n_blocks,
            out_specs=q_spec,
        ),
        compiler_params=pltpu.CompilerParams(
            dimension_semantics=("arbitrary", "arbitrary", "arbitrary")
        ),
        cost_estimate=pl.CostEstimate(
            flops=flops,
            transcendentals=local_pre * HQ * block_query * block * n_blocks,
            bytes_accessed=2 * pre_query.size * 2 + sum(b.size for b in kv_blocks) * 2,
        ),
    )(first_key, pre_query, *kv_blocks)


def body(
    pre_query,
    pre_fresh,
    pre_cache,
    pre_start,
    pre_resid,
    dec_query,
    dec_fresh,
    decode_window_cache,
    dec_length,
    dec_resid,
    out_weight,
    norm_gain,
    embedding,
):
    seq_count = lax.axis_size("seq")
    seq_index = lax.axis_index("seq")
    local_pre = pre_query.shape[0]
    block_query = pre_query.shape[1]
    score_scale = HEAD_SIZE ** (-0.5)
    kv_blocks = [None] * (seq_count + 1)
    kv_blocks[0] = pre_cache
    kv_blocks[seq_count] = pre_fresh
    for shift in range(1, seq_count):
        outgoing = jnp.where(seq_index + shift <= seq_count - 1, pre_fresh, pre_cache)
        kv_blocks[seq_count - shift] = from_behind(outgoing, "seq", shift)
    first_key = (WIN - seq_index * block_query - pre_start).astype(jnp.int32)
    pre_mixed_3d = prefill_attention(pre_query, kv_blocks, first_key)
    pre_mixed = pre_mixed_3d.reshape(local_pre * block_query, HQ * HEAD_SIZE)
    decode_token_rows = dec_query.reshape(-1, HQ, HEAD_SIZE)
    cache_scores = (
        jnp.einsum(
            "vfx,vzx->vfz",
            decode_token_rows,
            decode_window_cache[:, :, :HEAD_SIZE],
            preferred_element_type=jnp.float32,
        )
        * score_scale
    )
    self_scores = (
        jnp.einsum(
            "bhd,bd->bh",
            decode_token_rows,
            dec_fresh[:, :HEAD_SIZE],
            preferred_element_type=jnp.float32,
        )[:, :, None]
        * score_scale
    )
    slot_index = jnp.arange(WIN, dtype=jnp.int32)[None, :]
    length_col = dec_length[:, None]
    held_pos = length_col - 1 - jnp.mod(length_col - 1 - slot_index, WIN)
    live_mask = ((held_pos >= 0) & (held_pos > length_col - WIN))[:, None, :]
    peak_score = jnp.maximum(
        jnp.max(jnp.where(live_mask, cache_scores, NEG_BIG), axis=2, keepdims=True), self_scores
    )
    cache_attention_weights = jnp.where(live_mask, jnp.exp(cache_scores - peak_score), 0.0)
    self_weights = jnp.exp(self_scores - peak_score)
    denom_sum = jnp.sum(cache_attention_weights, axis=2, keepdims=True) + self_weights
    self_rounded = lax.optimization_barrier(self_weights.astype(jnp.bfloat16)).astype(jnp.float32)
    cache_part = jnp.einsum(
        "ect,ety->ecy",
        cache_attention_weights.astype(jnp.bfloat16),
        decode_window_cache[:, :, HEAD_SIZE:],
        preferred_element_type=jnp.float32,
    )
    self_part = self_rounded * dec_fresh[:, None, HEAD_SIZE:].astype(jnp.float32)
    dec_mixed = (
        ((cache_part + self_part) / denom_sum).astype(jnp.bfloat16).reshape(-1, HQ * HEAD_SIZE)
    )
    mixed_rows = jnp.concatenate([pre_mixed, dec_mixed], axis=0)
    projected = jnp.dot(
        mixed_rows,
        lax.all_gather(out_weight, "vocab", axis=0, tiled=True),
        preferred_element_type=jnp.float32,
    )
    pre_rows = local_pre * block_query
    pre_out = (
        pre_resid.astype(jnp.float32) + projected[:pre_rows].reshape(local_pre, block_query, D)
    ).astype(jnp.bfloat16)
    dec_out = (dec_resid.astype(jnp.float32) + projected[pre_rows:]).astype(jnp.bfloat16)
    local_dec = dec_mixed.shape[0]
    vocab_count = lax.axis_size("vocab")
    vocab_index = lax.axis_index("vocab")
    weight_rows = out_weight.shape[0]
    head_count = local_dec + local_pre
    head_mixed = jnp.concatenate([dec_mixed, pre_mixed_3d[:, block_query - 1, :]], axis=0)
    head_resid = jnp.concatenate([dec_resid, pre_resid[:, block_query - 1, :]], axis=0)
    column_blocks = head_mixed.reshape(head_count, vocab_count, weight_rows).transpose(1, 0, 2)
    own_columns = lax.all_to_all(column_blocks, "vocab", 0, 0, tiled=True).reshape(
        vocab_count * head_count, weight_rows
    )
    partial = jnp.dot(own_columns, out_weight, preferred_element_type=jnp.float32)
    pieces = lax.all_to_all(
        partial.reshape(vocab_count, head_count, D), "vocab", 0, 0, tiled=True
    )
    head_proj = jnp.sum(pieces, axis=0)
    head_in = (head_resid.astype(jnp.float32) + head_proj).astype(jnp.bfloat16)
    everyone = gather_all(normalize(head_in, norm_gain))
    layout = everyone.reshape(seq_count, vocab_count, head_count, D)
    decode_all = layout[:, :, :local_dec].reshape(-1, D)
    prefill_every_request = layout[seq_count - 1, :, local_dec:].reshape(-1, D)
    head_rows = jnp.concatenate([decode_all, prefill_every_request], axis=0)
    logits = lax.dot_general(
        head_rows, embedding, (((1,), (1,)), ((), ())), preferred_element_type=jnp.float32
    )
    local_peak = jnp.max(logits, axis=1)
    local_sum = jnp.sum(jnp.exp(logits - local_peak[:, None]), axis=1)
    own_stats = jnp.stack([local_peak, local_sum])[None]
    vocab_stats, (pre_out, dec_out) = doubling_gather(own_stats, "vocab", (pre_out, dec_out))
    stats, _ = doubling_gather(vocab_stats, "seq")
    global_peak = jnp.max(stats[:, 0], axis=0)
    global_sum = jnp.sum(stats[:, 1] * jnp.exp(stats[:, 0] - global_peak[None]), axis=0)
    total = (global_peak + jnp.log(global_sum))[:, None]
    log_probs = (logits - total).astype(jnp.bfloat16)
    dec_count = decode_all.shape[0]
    return (pre_out, dec_out, log_probs[:dec_count], log_probs[dec_count:])


def solution(mesh):
    in_specs = (
        P("vocab", "seq", None),
        P("vocab", "seq", None),
        P("vocab", "seq", None),
        P("vocab"),
        P("vocab", "seq", None),
        P(("seq", "vocab"), None),
        P(("seq", "vocab"), None),
        P(("seq", "vocab"), None, None),
        P(("seq", "vocab")),
        P(("seq", "vocab"), None),
        P("vocab", None),
        P(),
        P(("seq", "vocab"), None),
    )
    out_specs = (
        P("vocab", "seq", None),
        P(("seq", "vocab"), None),
        P(None, ("seq", "vocab")),
        P(None, ("seq", "vocab")),
    )
    return jax.shard_map(body, mesh=mesh, in_specs=in_specs, out_specs=out_specs, check_vma=False)
```

```python
import functools

import jax
import jax.numpy as jnp
from jax import lax
from jax.experimental import pallas as pl
from jax.experimental.pallas import tpu as pltpu
from jax.sharding import PartitionSpec as P

D = 2560
HQ = 10
HEAD_SIZE = 256
WIN = 2048


NEG_BIG = -1e30
STABILITY_FLOOR = 1e-06


def from_behind(value, axis, steps):
    count = lax.axis_size(axis)
    pairs = [(source, (source + steps) % count) for source in range(count)]
    return lax.ppermute(value, axis, pairs)


def gather_all(value):
    inner = lax.all_gather(value, "vocab", axis=0, tiled=True)
    return lax.all_gather(inner, "seq", axis=0, tiled=True)


def doubling_gather(value, axis, tie=None):
    count = lax.axis_size(axis)
    if count & (count - 1):
        return lax.all_gather(value, axis, axis=0, tiled=True), tie
    index = lax.axis_index(axis)
    tie_out = None
    step = 1
    while step < count:
        pairs = [(source, source ^ step) for source in range(count)]
        theirs = lax.ppermute(value, axis, pairs)
        if tie is not None:
            theirs, tie = lax.optimization_barrier((theirs, tie))
            tie_out, tie = tie, None
        upper = (index // step) % 2 == 1
        value = jnp.where(
            upper,
            jnp.concatenate([theirs, value], axis=0),
            jnp.concatenate([value, theirs], axis=0),
        )
        step *= 2
    if tie is not None:
        return value, tie
    return value, tie_out


def normalize(rows_in, gain):
    values = rows_in.astype(jnp.float32)
    square_mean = jnp.mean(values * values, axis=-1, keepdims=True)
    return (values * lax.rsqrt(square_mean + STABILITY_FLOOR) * gain).astype(jnp.bfloat16)


def prefill_kernel(t0_ref, q_ref, *refs, n_blocks, block, tq):
    kv_refs = refs[:n_blocks]
    o_ref = refs[n_blocks]
    r = pl.program_id(0)
    qi = pl.program_id(2)
    t0 = t0_ref[r]
    q = q_ref[0]
    row = qi * tq + lax.broadcasted_iota(jnp.int32, (tq, block), 0)
    col = lax.broadcasted_iota(jnp.int32, (tq, block), 1)
    peak = jnp.full((tq, 1), NEG_BIG, jnp.float32)
    denom = jnp.zeros((tq, 1), jnp.float32)
    accum = jnp.zeros((tq, HEAD_SIZE), jnp.float32)
    scale = HEAD_SIZE ** (-0.5)
    for j in range(n_blocks):
        kv = kv_refs[j]
        keys = kv[0, :, :HEAD_SIZE]
        values = kv[0, :, HEAD_SIZE:]
        scores = (
            lax.dot_general(
                q, keys, (((1,), (1,)), ((), ())), preferred_element_type=jnp.float32
            )
            * scale
        )
        t = j * block + col
        if j == 0 or j == n_blocks - 1:
            valid = t >= t0
            if j == 0:
                valid = valid & (t > row)
            else:
                valid = valid & (t <= row + WIN)
            scores = jnp.where(valid, scores, NEG_BIG)
        else:
            key = j * block + lax.broadcasted_iota(jnp.int32, (1, block), 1)
            scores = scores + jnp.where(key >= t0, 0.0, NEG_BIG)
        peak_new = jnp.maximum(peak, jnp.max(scores, axis=1, keepdims=True))
        weights = jnp.exp(scores - peak_new)
        decay = jnp.exp(peak - peak_new)
        denom = denom * decay + jnp.sum(weights, axis=1, keepdims=True)
        accum = accum * decay + jnp.dot(
            weights.astype(jnp.bfloat16), values, preferred_element_type=jnp.float32
        )
        peak = peak_new
    o_ref[0] = (accum / denom).astype(o_ref.dtype)


def prefill_attention(pre_query, kv_blocks, first_key):
    local_pre, block_query, _ = pre_query.shape
    block = kv_blocks[0].shape[1]
    n_blocks = len(kv_blocks)
    tq = min(block_query, 512)
    kernel = functools.partial(prefill_kernel, n_blocks=n_blocks, block=block, tq=tq)
    kv_spec = pl.BlockSpec((1, block, 2 * HEAD_SIZE), lambda r, h, qi, t0: (r, 0, 0))
    q_spec = pl.BlockSpec((1, tq, HEAD_SIZE), lambda r, h, qi, t0: (r, qi, h))
    flops = 4 * local_pre * HQ * block_query * block * n_blocks * HEAD_SIZE
    return pl.pallas_call(
        kernel,
        out_shape=jax.ShapeDtypeStruct(pre_query.shape, jnp.bfloat16),
        grid_spec=pltpu.PrefetchScalarGridSpec(
            num_scalar_prefetch=1,
            grid=(local_pre, HQ, block_query // tq),
            in_specs=[q_spec] + [kv_spec] * n_blocks,
            out_specs=q_spec,
        ),
        compiler_params=pltpu.CompilerParams(
            dimension_semantics=("arbitrary", "arbitrary", "arbitrary")
        ),
        cost_estimate=pl.CostEstimate(
            flops=flops,
            transcendentals=local_pre * HQ * block_query * block * n_blocks,
            bytes_accessed=2 * pre_query.size * 2 + sum(b.size for b in kv_blocks) * 2,
        ),
    )(first_key, pre_query, *kv_blocks)


def body(
    pre_query,
    pre_fresh,
    pre_cache,
    pre_start,
    pre_resid,
    dec_query,
    dec_fresh,
    decode_window_cache,
    dec_length,
    dec_resid,
    out_weight,
    norm_gain,
    embedding,
):
    seq_count = lax.axis_size("seq")
    seq_index = lax.axis_index("seq")
    local_pre = pre_query.shape[0]
    block_query = pre_query.shape[1]
    score_scale = HEAD_SIZE ** (-0.5)
    kv_blocks = [None] * (seq_count + 1)
    kv_blocks[0] = pre_cache
    kv_blocks[seq_count] = pre_fresh
    for shift in range(1, seq_count):
        outgoing = jnp.where(seq_index + shift <= seq_count - 1, pre_fresh, pre_cache)
        kv_blocks[seq_count - shift] = from_behind(outgoing, "seq", shift)
    first_key = (WIN - seq_index * block_query - pre_start).astype(jnp.int32)
    pre_mixed_3d = prefill_attention(pre_query, kv_blocks, first_key)
    pre_mixed = pre_mixed_3d.reshape(local_pre * block_query, HQ * HEAD_SIZE)
    decode_token_rows = dec_query.reshape(-1, HQ, HEAD_SIZE)
    cache_scores = (
        jnp.einsum(
            "vfx,vzx->vfz",
            decode_token_rows,
            decode_window_cache[:, :, :HEAD_SIZE],
            preferred_element_type=jnp.float32,
        )
        * score_scale
    )
    self_scores = (
        jnp.einsum(
            "bhd,bd->bh",
            decode_token_rows,
            dec_fresh[:, :HEAD_SIZE],
            preferred_element_type=jnp.float32,
        )[:, :, None]
        * score_scale
    )
    slot_index = jnp.arange(WIN, dtype=jnp.int32)[None, :]
    length_col = dec_length[:, None]
    held_pos = length_col - 1 - jnp.mod(length_col - 1 - slot_index, WIN)
    live_mask = ((held_pos >= 0) & (held_pos > length_col - WIN))[:, None, :]
    peak_score = jnp.maximum(
        jnp.max(jnp.where(live_mask, cache_scores, NEG_BIG), axis=2, keepdims=True), self_scores
    )
    cache_attention_weights = jnp.where(live_mask, jnp.exp(cache_scores - peak_score), 0.0)
    self_weights = jnp.exp(self_scores - peak_score)
    denom_sum = jnp.sum(cache_attention_weights, axis=2, keepdims=True) + self_weights
    self_rounded = lax.optimization_barrier(self_weights.astype(jnp.bfloat16)).astype(jnp.float32)
    cache_part = jnp.einsum(
        "ect,ety->ecy",
        cache_attention_weights.astype(jnp.bfloat16),
        decode_window_cache[:, :, HEAD_SIZE:],
        preferred_element_type=jnp.float32,
    )
    self_part = self_rounded * dec_fresh[:, None, HEAD_SIZE:].astype(jnp.float32)
    dec_mixed = (
        ((cache_part + self_part) / denom_sum).astype(jnp.bfloat16).reshape(-1, HQ * HEAD_SIZE)
    )
    mixed_rows = jnp.concatenate([pre_mixed, dec_mixed], axis=0)
    projected = jnp.dot(
        mixed_rows,
        lax.all_gather(out_weight, "vocab", axis=0, tiled=True),
        preferred_element_type=jnp.float32,
    )
    pre_rows = local_pre * block_query
    pre_out = (
        pre_resid.astype(jnp.float32) + projected[:pre_rows].reshape(local_pre, block_query, D)
    ).astype(jnp.bfloat16)
    dec_out = (dec_resid.astype(jnp.float32) + projected[pre_rows:]).astype(jnp.bfloat16)
    local_dec = dec_mixed.shape[0]
    vocab_count = lax.axis_size("vocab")
    vocab_index = lax.axis_index("vocab")
    weight_rows = out_weight.shape[0]
    head_count = local_dec + local_pre
    head_mixed = jnp.concatenate([dec_mixed, pre_mixed_3d[:, block_query - 1, :]], axis=0)
    head_resid = jnp.concatenate([dec_resid, pre_resid[:, block_query - 1, :]], axis=0)
    column_blocks = head_mixed.reshape(head_count, vocab_count, weight_rows).transpose(1, 0, 2)
    own_columns = lax.all_to_all(column_blocks, "vocab", 0, 0, tiled=True).reshape(
        vocab_count * head_count, weight_rows
    )
    partial = jnp.dot(own_columns, out_weight, preferred_element_type=jnp.float32)
    pieces = lax.all_to_all(
        partial.reshape(vocab_count, head_count, D), "vocab", 0, 0, tiled=True
    )
    head_proj = jnp.sum(pieces, axis=0)
    head_in = (head_resid.astype(jnp.float32) + head_proj).astype(jnp.bfloat16)
    by_seq = lax.all_gather(normalize(head_in, norm_gain), "seq", axis=0, tiled=True)
    everyone = lax.all_gather(by_seq, "vocab", axis=0, tiled=True)
    layout = everyone.reshape(vocab_count, seq_count, head_count, D).transpose(1, 0, 2, 3)
    decode_all = layout[:, :, :local_dec].reshape(-1, D)
    prefill_every_request = layout[seq_count - 1, :, local_dec:].reshape(-1, D)
    head_rows = jnp.concatenate([decode_all, prefill_every_request], axis=0)
    logits = lax.dot_general(
        head_rows, embedding, (((1,), (1,)), ((), ())), preferred_element_type=jnp.float32
    )
    local_peak = jnp.max(logits, axis=1)
    local_sum = jnp.sum(jnp.exp(logits - local_peak[:, None]), axis=1)
    own_stats = jnp.stack([local_peak, local_sum])[None]
    vocab_stats, (pre_out, dec_out) = doubling_gather(own_stats, "vocab", (pre_out, dec_out))
    stats, _ = doubling_gather(vocab_stats, "seq")
    global_peak = jnp.max(stats[:, 0], axis=0)
    global_sum = jnp.sum(stats[:, 1] * jnp.exp(stats[:, 0] - global_peak[None]), axis=0)
    total = (global_peak + jnp.log(global_sum))[:, None]
    log_probs = (logits - total).astype(jnp.bfloat16)
    dec_count = decode_all.shape[0]
    return (pre_out, dec_out, log_probs[:dec_count], log_probs[dec_count:])


def solution(mesh):
    in_specs = (
        P("vocab", "seq", None),
        P("vocab", "seq", None),
        P("vocab", "seq", None),
        P("vocab"),
        P("vocab", "seq", None),
        P(("seq", "vocab"), None),
        P(("seq", "vocab"), None),
        P(("seq", "vocab"), None, None),
        P(("seq", "vocab")),
        P(("seq", "vocab"), None),
        P("vocab", None),
        P(),
        P(("seq", "vocab"), None),
    )
    out_specs = (
        P("vocab", "seq", None),
        P(("seq", "vocab"), None),
        P(None, ("seq", "vocab")),
        P(None, ("seq", "vocab")),
    )
    return jax.shard_map(body, mesh=mesh, in_specs=in_specs, out_specs=out_specs, check_vma=False)
```
